32 devices in a mesh: grp: 2 (over x), blk: 16 (over z, y, core).
Axes of the slice: x: 2, y: 2, z: 4, core: 2. Of those that a mesh axis runs over, the one named last changes fastest.
Arguments:
- tokens: bfloat16 [16384, 1024], P(('grp', 'blk')), parts along dimension 0, may hold values from -6 to 6
- patch_of_row: int32 [16384], P(('grp', 'blk')), parts along dimension 0, may hold values from 0 to 2047, as said below
- latents: bfloat16 [256, 1024], P('blk'), may hold values from -110 to 110
- contrast_gain: bfloat16 [4, 1024], replicated, may hold values from 0.099609375 to 1.8984375
- norm_gain: bfloat16 [1024], replicated, may hold values from 0.099609375 to 1.8984375
- w_query: bfloat16 [1024, 1024], replicated, may hold values from -0.1875 to 0.1875
- w_key: bfloat16 [1024, 1024], replicated, may hold values from -0.1875 to 0.1875
- w_value: bfloat16 [1024, 1024], replicated, may hold values from -0.1875 to 0.1875
- w_out: bfloat16 [1024, 1024], replicated, may hold values from -0.1875 to 0.1875
Outputs:
- new_latents: bfloat16 [512, 1024], P(('grp', 'blk')), parts along dimension 0
The draws below stay inside these ranges and needn't reach their ends.
There are 2 independent parts, one for each index of `grp`. The reference program is written for one: setup_inputs(seed, part) draws one part's arguments, and reference() takes and returns one part's arrays. A program takes and returns all parts, laid end to end along the dimension named above; an argument that names none is the same for every part. Nothing has to cross between parts.
Inputs may be any that keep to these rules, and one draw needn't show every extreme that they name: `patch_of_row`: for each contrast c, rows c * 2048 to (c + 1) * 2048 - 1 name every patch once, and row c * 2048 + s names a patch p with p // 128 == s % 16.
All inputs are finite; a program needn't handle non-finite values.
Results may differ from the reference program's by a relative error of at most 0.0065.
Values may be sent and summed in bfloat16 or wider, within the bound.
No kernel may reach another device: no remote copies, remote signals or barrier semaphores. Data moves between devices by JAX's collectives and lax.ppermute only.
A program may use at most 64 MiB of HBM per device.

```python
import jax
import jax.numpy as jnp
from jax import lax

D = 1024
HEADS = 16
CONTRASTS = 4
PATCH_DEV = 128
LAT_DEV = 16
HD = 64
PATCHES = 2048
ROWS = 8192
LATENTS = 256
N_BLK = 16


def draw_latents(key, part):
    normal_part = jax.random.normal(jax.random.fold_in(key, 13), (LATENTS, D), jnp.float32)
    return (3.0 * jnp.clip(normal_part, -6.0, 6.0)).astype(jnp.bfloat16)


def draw_patch_of_row(key, part):
    raw_scores = jax.random.randint(key, (CONTRASTS, N_BLK, PATCH_DEV), 0, 524288)
    offsets = jnp.arange(PATCH_DEV, dtype=jnp.int32)[None, None, :]
    distinct = raw_scores * PATCH_DEV + offsets
    ranking = jnp.argsort(distinct, axis=-1, stable=True).astype(jnp.int32)
    owners = jnp.arange(N_BLK, dtype=jnp.int32)[None, :, None] * PATCH_DEV
    patches = owners + ranking
    return jnp.transpose(patches, (0, 2, 1)).reshape(CONTRASTS * PATCH_DEV * N_BLK).astype(jnp.int32)


def steps_of(key, extent, pieces, low, largest):
    gain, own = 1.0, jax.random.fold_in(key, 6)
    for axis_at, parts in pieces:
        steps = jnp.exp(jax.random.uniform(jax.random.fold_in(own, axis_at), (parts,), jnp.float32, low / len(pieces), largest / len(pieces)))
        gain = gain * jnp.repeat(steps, extent[axis_at] // parts).reshape([-1 if axis == axis_at else 1 for axis in range(len(extent))])
    return gain


def noise(stream_key, dims, scale, reach, cuts=(), held_as=jnp.bfloat16):
    values = scale * jax.random.normal(stream_key, dims, jnp.float32)
    if cuts:
        values = values * steps_of(stream_key, dims, cuts, -0.22, 0.18)
    return jnp.clip(values, -reach, reach).astype(held_as)


def setup_inputs(seed: int = 0, part: int = 0) -> dict:
    key_of = jax.random.split(jax.random.key(seed), 10)
    own_keys = jax.random.split(jax.random.fold_in(key_of[9], part), 10)
    tokens = noise(own_keys[0], (ROWS, D), 1.0, 6.0, ((0, 16),))
    patch_of_row = draw_patch_of_row(jax.random.fold_in(jax.random.fold_in(key_of[9], part), 71), part)
    latents = draw_latents(jax.random.fold_in(key_of[9], 71), part)
    contrast_gain = jnp.clip(1.0 + 0.18 * jax.random.normal(key_of[3], (CONTRASTS, D), jnp.float32), 0.099609375, 1.8984375).astype(jnp.bfloat16)
    norm_gain = jnp.clip(1.0 + 0.18 * jax.random.normal(key_of[4], (D,), jnp.float32), 0.099609375, 1.8984375).astype(jnp.bfloat16)
    w_query = noise(key_of[5], (D, D), D ** -0.5, 0.1875)
    w_key = noise(key_of[6], (D, D), D ** -0.5, 0.1875)
    w_value = noise(key_of[7], (D, D), D ** -0.5, 0.1875)
    w_out = noise(key_of[8], (D, D), D ** -0.5, 0.1875)
    return {"tokens": tokens, "patch_of_row": patch_of_row, "latents": latents, "contrast_gain": contrast_gain, "norm_gain": norm_gain, "w_query": w_query, "w_key": w_key, "w_value": w_value, "w_out": w_out}


def reference(tokens, patch_of_row, latents, contrast_gain, norm_gain, w_query, w_key, w_value, w_out):
    contrast_id = jnp.arange(ROWS, dtype=jnp.int32) // PATCHES
    scaled = tokens.astype(jnp.float32) * contrast_gain.astype(jnp.float32)[contrast_id]
    joined = jnp.zeros((PATCHES, D), jnp.float32).at[patch_of_row].add(scaled)
    inverse_rms = lax.rsqrt(lax.optimization_barrier(jnp.mean(joined * joined, axis=-1, keepdims=True)) + 1e-05)
    normed = (joined * inverse_rms * norm_gain.astype(jnp.float32)).astype(jnp.bfloat16)
    key_rows = jnp.dot(normed, w_key, preferred_element_type=jnp.float32).astype(jnp.bfloat16)
    value_rows = jnp.dot(normed, w_value, preferred_element_type=jnp.float32).astype(jnp.bfloat16)
    queries = (jnp.dot(latents, w_query, preferred_element_type=jnp.float32) * HD ** (-0.5)).astype(jnp.bfloat16)
    key_heads = key_rows.astype(jnp.float32).reshape(PATCHES, HEADS, HD)
    value_heads = value_rows.astype(jnp.float32).reshape(PATCHES, HEADS, HD)

    def attend(query_block):
        block_rows = query_block.shape[0]
        query_heads = query_block.astype(jnp.float32).reshape(block_rows, HEADS, HD)
        scores = jnp.einsum('bhd,khd->bhk', query_heads, key_heads)
        maxima = lax.optimization_barrier(jnp.max(scores, axis=-1))
        weights = jnp.exp(scores - maxima[..., None])
        totals = lax.optimization_barrier(jnp.sum(weights, axis=-1))
        rounded = lax.optimization_barrier(weights.astype(jnp.bfloat16)).astype(jnp.float32)
        summed = jnp.einsum('bhk,khd->bhd', rounded, value_heads)
        return (summed / totals[..., None]).reshape(block_rows, D).astype(jnp.bfloat16)
    attended = lax.map(attend, queries.reshape(LATENTS // LAT_DEV, LAT_DEV, D)).reshape(LATENTS, D)
    mixed = latents.astype(jnp.float32) + jnp.dot(attended, w_out, preferred_element_type=jnp.float32)
    return mixed.astype(jnp.bfloat16)
```

```python
import jax
import jax.numpy as jnp
from jax import lax
from jax.sharding import PartitionSpec as P

HEADS = 16
CONTRASTS = 4


def split_exact(value, upward):
    high = value.astype(jnp.bfloat16)
    rest = value - high.astype(jnp.float32)
    if upward:
        rest = rest + jnp.abs(rest) * (2.0 ** -8)
    low = rest.astype(jnp.bfloat16)
    return high, low


def joined_rows(tokens, patch_of_row, contrast_gain, cycle_size, my_index):
    tok_rows, model_width = tokens.shape
    per_peer = tok_rows // cycle_size
    patches_dev = tok_rows // CONTRASTS
    all_ids = lax.all_gather(patch_of_row, "blk", tiled=True)
    received = lax.all_to_all(
        tokens.reshape(per_peer, cycle_size, model_width),
        "blk",
        split_axis=1,
        concat_axis=1,
        tiled=True,
    )
    received_ids = jnp.transpose(
        lax.dynamic_index_in_dim(
            all_ids.reshape(cycle_size, per_peer, cycle_size), my_index, axis=2, keepdims=False
        )
    )
    source_dev = lax.broadcasted_iota(jnp.int32, (per_peer, cycle_size), 1)
    row_step = lax.broadcasted_iota(jnp.int32, (per_peer, cycle_size), 0)
    slot_index = source_dev * tok_rows + my_index + cycle_size * row_step
    contrast_id = slot_index // (patches_dev * cycle_size)
    target_row = (contrast_id * patches_dev + received_ids - my_index * patches_dev).reshape(
        tok_rows
    )
    inverse = (
        jnp.zeros((tok_rows,), jnp.int32).at[target_row].set(jnp.arange(tok_rows, dtype=jnp.int32))
    )
    arranged = received.reshape(tok_rows, model_width)[inverse].reshape(
        CONTRASTS, patches_dev, model_width
    )
    return jnp.sum(
        arranged.astype(jnp.float32) * contrast_gain.astype(jnp.float32)[:, None, :], axis=0
    )


def local(tokens, patch_of_row, latents, contrast_gain, norm_gain, w_query, w_key, w_value, w_out):
    cycle_size = lax.axis_size("blk")
    my_index = lax.axis_index("blk")
    model_width = tokens.shape[1]
    head_count = HEADS
    head_width = model_width // head_count
    lat_rows = latents.shape[0]

    queries = (
        jnp.dot(latents, w_query, preferred_element_type=jnp.float32) * head_width ** (-0.5)
    ).astype(jnp.bfloat16)
    all_queries = lax.all_gather(queries, "blk", tiled=True)
    all_lat = all_queries.shape[0]

    joined = joined_rows(tokens, patch_of_row, contrast_gain, cycle_size, my_index)
    patches_dev = joined.shape[0]
    inverse_rms = lax.rsqrt(jnp.mean(joined * joined, axis=-1, keepdims=True) + 1e-05)
    normed = (joined * inverse_rms * norm_gain.astype(jnp.float32)).astype(jnp.bfloat16)
    key_rows = jnp.dot(normed, w_key, preferred_element_type=jnp.float32).astype(jnp.bfloat16)
    value_rows = jnp.dot(normed, w_value, preferred_element_type=jnp.float32).astype(jnp.bfloat16)
    key_heads = key_rows.reshape(patches_dev, head_count, head_width)
    value_heads = value_rows.reshape(patches_dev, head_count, head_width)

    query_heads = all_queries.reshape(all_lat, head_count, head_width)
    scores = jnp.einsum(
        "lhd,khd->lhk", query_heads, key_heads, preferred_element_type=jnp.float32
    )
    maxima = jnp.max(scores, axis=-1)
    max_high, max_low = split_exact(maxima, True)
    shift = max_high.astype(jnp.float32) + max_low.astype(jnp.float32)
    weights = jnp.exp(scores - shift[..., None])
    totals = jnp.sum(weights, axis=-1)
    tot_high, tot_low = split_exact(totals, False)
    summed = jnp.einsum(
        "lhk,khd->lhd",
        weights.astype(jnp.bfloat16),
        value_heads,
        preferred_element_type=jnp.float32,
    )
    stats = jnp.stack([max_high, max_low, tot_high, tot_low], axis=-1).reshape(
        cycle_size, lat_rows, head_count * 4
    )
    payload = jnp.concatenate(
        [summed.astype(jnp.bfloat16).reshape(cycle_size, lat_rows, model_width), stats], axis=-1
    )
    gathered = lax.all_to_all(payload, "blk", split_axis=0, concat_axis=0, tiled=True)
    part_sums = gathered[:, :, :model_width].astype(jnp.float32).reshape(
        cycle_size, lat_rows, head_count, head_width
    )
    part_stats = gathered[:, :, model_width:].astype(jnp.float32).reshape(
        cycle_size, lat_rows, head_count, 4
    )
    part_max = part_stats[..., 0] + part_stats[..., 1]
    part_tot = part_stats[..., 2] + part_stats[..., 3]
    top = jnp.max(part_max, axis=0)
    factor = jnp.exp(part_max - top[None])
    total = jnp.sum(part_tot * factor, axis=0)
    accum = jnp.sum(part_sums * factor[..., None], axis=0)
    attended = (accum / total[..., None]).reshape(lat_rows, model_width).astype(jnp.bfloat16)
    mixed = latents.astype(jnp.float32) + jnp.dot(
        attended, w_out, preferred_element_type=jnp.float32
    )
    return mixed.astype(jnp.bfloat16)


def solution(mesh):
    in_specs = (
        P(("grp", "blk"), None),
        P(("grp", "blk")),
        P("blk", None),
        P(),
        P(),
        P(),
        P(),
        P(),
        P(),
    )
    out_specs = P(("grp", "blk"), None)
    return jax.shard_map(local, mesh=mesh, in_specs=in_specs, out_specs=out_specs, check_vma=False)
```

```python
import jax
import jax.numpy as jnp
from jax import lax
from jax.sharding import PartitionSpec as P

HEADS = 16
CONTRASTS = 4


def joined_rows(tokens, patch_of_row, contrast_gain, cycle_size, my_index):
    tok_rows, model_width = tokens.shape
    per_peer = tok_rows // cycle_size
    patches_dev = tok_rows // CONTRASTS
    all_ids = lax.all_gather(patch_of_row, "blk", tiled=True)
    received = lax.all_to_all(
        tokens.reshape(per_peer, cycle_size, model_width),
        "blk",
        split_axis=1,
        concat_axis=1,
        tiled=True,
    )
    received_ids = jnp.transpose(
        lax.dynamic_index_in_dim(
            all_ids.reshape(cycle_size, per_peer, cycle_size), my_index, axis=2, keepdims=False
        )
    )
    source_dev = lax.broadcasted_iota(jnp.int32, (per_peer, cycle_size), 1)
    row_step = lax.broadcasted_iota(jnp.int32, (per_peer, cycle_size), 0)
    slot_index = source_dev * tok_rows + my_index + cycle_size * row_step
    contrast_id = slot_index // (patches_dev * cycle_size)
    target_row = (contrast_id * patches_dev + received_ids - my_index * patches_dev).reshape(
        tok_rows
    )
    inverse = (
        jnp.zeros((tok_rows,), jnp.int32).at[target_row].set(jnp.arange(tok_rows, dtype=jnp.int32))
    )
    arranged = received.reshape(tok_rows, model_width)[inverse].reshape(
        CONTRASTS, patches_dev, model_width
    )
    return jnp.sum(
        arranged.astype(jnp.float32) * contrast_gain.astype(jnp.float32)[:, None, :], axis=0
    )


def local(tokens, patch_of_row, latents, contrast_gain, norm_gain, w_query, w_key, w_value, w_out):
    cycle_size = lax.axis_size("blk")
    my_index = lax.axis_index("blk")
    model_width = tokens.shape[1]
    head_count = HEADS
    head_width = model_width // head_count
    lat_rows = latents.shape[0]
    copies = cycle_size // head_count
    group_start = (my_index // head_count) * head_count

    queries = (
        jnp.dot(latents, w_query, preferred_element_type=jnp.float32) * head_width ** (-0.5)
    ).astype(jnp.bfloat16)
    query_parts = jnp.transpose(queries.reshape(lat_rows, head_count, head_width), (1, 0, 2))
    got_queries = lax.all_to_all(
        jnp.tile(query_parts, (copies, 1, 1)), "blk", split_axis=0, concat_axis=0, tiled=True
    )
    head_queries = lax.dynamic_slice_in_dim(got_queries, group_start, head_count, axis=0).reshape(
        head_count * lat_rows, head_width
    )

    joined = joined_rows(tokens, patch_of_row, contrast_gain, cycle_size, my_index)
    patches_dev = joined.shape[0]
    inverse_rms = lax.rsqrt(jnp.mean(joined * joined, axis=-1, keepdims=True) + 1e-05)
    normed = (joined * inverse_rms * norm_gain.astype(jnp.float32)).astype(jnp.bfloat16)
    key_rows = jnp.dot(normed, w_key, preferred_element_type=jnp.float32).astype(jnp.bfloat16)
    value_rows = jnp.dot(normed, w_value, preferred_element_type=jnp.float32).astype(jnp.bfloat16)
    pair_parts = jnp.transpose(
        jnp.concatenate(
            [
                key_rows.reshape(patches_dev, head_count, head_width),
                value_rows.reshape(patches_dev, head_count, head_width),
            ],
            axis=-1,
        ),
        (1, 0, 2),
    )
    got_pairs = lax.all_to_all(
        jnp.tile(pair_parts, (copies, 1, 1)), "blk", split_axis=0, concat_axis=0, tiled=True
    ).reshape(cycle_size * patches_dev, 2 * head_width)
    head_keys = got_pairs[:, :head_width]
    head_values = got_pairs[:, head_width:]

    scores = jnp.einsum(
        "ld,kd->lk", head_queries, head_keys, preferred_element_type=jnp.float32
    )
    maxima = jnp.max(scores, axis=-1, keepdims=True)
    weights = jnp.exp(scores - maxima)
    totals = jnp.sum(weights, axis=-1, keepdims=True)
    summed = jnp.dot(weights.astype(jnp.bfloat16), head_values, preferred_element_type=jnp.float32)
    attended_head = (summed / totals).astype(jnp.bfloat16).reshape(head_count, lat_rows, head_width)
    got_attended = lax.all_to_all(
        jnp.tile(attended_head, (copies, 1, 1)), "blk", split_axis=0, concat_axis=0, tiled=True
    )
    attended = jnp.transpose(
        lax.dynamic_slice_in_dim(got_attended, group_start, head_count, axis=0), (1, 0, 2)
    ).reshape(lat_rows, model_width)
    mixed = latents.astype(jnp.float32) + jnp.dot(
        attended, w_out, preferred_element_type=jnp.float32
    )
    return mixed.astype(jnp.bfloat16)


def solution(mesh):
    in_specs = (
        P(("grp", "blk"), None),
        P(("grp", "blk")),
        P("blk", None),
        P(),
        P(),
        P(),
        P(),
        P(),
        P(),
    )
    out_specs = P(("grp", "blk"), None)
    return jax.shard_map(local, mesh=mesh, in_specs=in_specs, out_specs=out_specs, check_vma=False)
```

```python
import jax
import jax.numpy as jnp
from jax import lax
from jax.sharding import PartitionSpec as P

HEADS = 16
CONTRASTS = 4


def local(tokens, patch_of_row, latents, contrast_gain, norm_gain, w_query, w_key, w_value, w_out):
    cycle_size = lax.axis_size("blk")
    my_index = lax.axis_index("blk")
    tok_rows, model_width = tokens.shape
    head_count = HEADS
    head_width = model_width // head_count
    lat_rows = latents.shape[0]
    copies = cycle_size // head_count
    group_start = (my_index // head_count) * head_count
    per_peer = tok_rows // cycle_size
    patches_dev = tok_rows // CONTRASTS
    lanes = 128

    queries = (
        jnp.dot(latents, w_query, preferred_element_type=jnp.float32) * head_width ** (-0.5)
    ).astype(jnp.bfloat16)
    query_parts = jnp.tile(
        jnp.transpose(queries.reshape(lat_rows, head_count, head_width), (1, 0, 2)),
        (copies, 1, 1),
    ).reshape(cycle_size, -1, lanes)
    token_parts = jnp.transpose(
        tokens.reshape(per_peer, cycle_size, model_width), (1, 0, 2)
    ).reshape(cycle_size, -1, lanes)
    row_dest = lax.broadcasted_iota(jnp.int32, (tok_rows,), 0) % cycle_size
    local_ids = (patch_of_row - row_dest * patches_dev).astype(jnp.bfloat16)
    id_parts = jnp.transpose(local_ids.reshape(per_peer, cycle_size))
    id_width = -(-per_peer // lanes) * lanes
    id_parts = jnp.pad(id_parts, ((0, 0), (0, id_width - per_peer))).reshape(cycle_size, -1, lanes)
    token_len = token_parts.shape[1]
    query_len = query_parts.shape[1]
    payload = jnp.concatenate([token_parts, query_parts, id_parts], axis=1)
    got = lax.all_to_all(payload, "blk", split_axis=0, concat_axis=0, tiled=True)

    head_queries = lax.dynamic_slice_in_dim(
        got[:, token_len : token_len + query_len], group_start, head_count, axis=0
    ).reshape(head_count * lat_rows, head_width)
    recv_rows = got[:, :token_len].reshape(CONTRASTS, patches_dev, model_width)
    recv_ids = (
        got[:, token_len + query_len :].reshape(cycle_size, id_width)[:, :per_peer]
        .astype(jnp.int32)
        .reshape(CONTRASTS, 1, patches_dev)
    )
    patch_iota = lax.broadcasted_iota(jnp.int32, (CONTRASTS, patches_dev, patches_dev), 1)
    selector = (recv_ids == patch_iota).astype(jnp.bfloat16)
    arranged = jnp.einsum(
        "cpk,ckd->cpd", selector, recv_rows, preferred_element_type=jnp.float32
    )
    joined = jnp.sum(arranged * contrast_gain.astype(jnp.float32)[:, None, :], axis=0)

    inverse_rms = lax.rsqrt(jnp.mean(joined * joined, axis=-1, keepdims=True) + 1e-05)
    normed = (joined * inverse_rms * norm_gain.astype(jnp.float32)).astype(jnp.bfloat16)
    key_rows = jnp.dot(normed, w_key, preferred_element_type=jnp.float32).astype(jnp.bfloat16)
    value_rows = jnp.dot(normed, w_value, preferred_element_type=jnp.float32).astype(jnp.bfloat16)
    pair_parts = jnp.transpose(
        jnp.concatenate(
            [
                key_rows.reshape(patches_dev, head_count, head_width),
                value_rows.reshape(patches_dev, head_count, head_width),
            ],
            axis=-1,
        ),
        (1, 0, 2),
    )
    got_pairs = lax.all_to_all(
        jnp.tile(pair_parts, (copies, 1, 1)), "blk", split_axis=0, concat_axis=0, tiled=True
    ).reshape(cycle_size * patches_dev, 2 * head_width)
    head_keys = got_pairs[:, :head_width]
    head_values = got_pairs[:, head_width:]

    scores = jnp.einsum(
        "ld,kd->lk", head_queries, head_keys, preferred_element_type=jnp.float32
    )
    maxima = jnp.max(scores, axis=-1, keepdims=True)
    weights = jnp.exp(scores - maxima)
    totals = jnp.sum(weights, axis=-1, keepdims=True)
    summed = jnp.dot(weights.astype(jnp.bfloat16), head_values, preferred_element_type=jnp.float32)
    attended_head = (summed / totals).astype(jnp.bfloat16).reshape(head_count, lat_rows, head_width)
    got_attended = lax.all_to_all(
        jnp.tile(attended_head, (copies, 1, 1)), "blk", split_axis=0, concat_axis=0, tiled=True
    )
    attended = jnp.transpose(
        lax.dynamic_slice_in_dim(got_attended, group_start, head_count, axis=0), (1, 0, 2)
    ).reshape(lat_rows, model_width)
    mixed = latents.astype(jnp.float32) + jnp.dot(
        attended, w_out, preferred_element_type=jnp.float32
    )
    return mixed.astype(jnp.bfloat16)


def solution(mesh):
    in_specs = (
        P(("grp", "blk"), None),
        P(("grp", "blk")),
        P("blk", None),
        P(),
        P(),
        P(),
        P(),
        P(),
        P(),
    )
    out_specs = P(("grp", "blk"), None)
    return jax.shard_map(local, mesh=mesh, in_specs=in_specs, out_specs=out_specs, check_vma=False)
```

```python
import jax
import jax.numpy as jnp
from jax import lax
from jax.sharding import PartitionSpec as P

HEADS = 16
CONTRASTS = 4


def local(tokens, patch_of_row, latents, contrast_gain, norm_gain, w_query, w_key, w_value, w_out):
    cycle_size = lax.axis_size("blk")
    my_index = lax.axis_index("blk")
    tok_rows, model_width = tokens.shape
    head_count = HEADS
    head_width = model_width // head_count
    lat_rows = latents.shape[0]
    copies = cycle_size // head_count
    group_start = (my_index // head_count) * head_count
    per_peer = tok_rows // cycle_size
    patches_dev = tok_rows // CONTRASTS
    lanes = 128

    queries = (
        jnp.dot(latents, w_query, preferred_element_type=jnp.float32) * head_width ** (-0.5)
    ).astype(jnp.bfloat16)
    token_parts = jnp.transpose(
        tokens.reshape(per_peer, cycle_size, model_width), (1, 0, 2)
    ).reshape(cycle_size, -1, lanes)
    row_dest = lax.broadcasted_iota(jnp.int32, (tok_rows,), 0) % cycle_size
    local_ids = (patch_of_row - row_dest * patches_dev).astype(jnp.bfloat16)
    id_parts = jnp.transpose(local_ids.reshape(per_peer, cycle_size))
    id_width = -(-per_peer // lanes) * lanes
    id_parts = jnp.pad(id_parts, ((0, 0), (0, id_width - per_peer))).reshape(cycle_size, -1, lanes)
    token_len = token_parts.shape[1]
    payload = jnp.concatenate([token_parts, id_parts], axis=1)
    got = lax.all_to_all(payload, "blk", split_axis=0, concat_axis=0, tiled=True)

    recv_rows = got[:, :token_len].reshape(CONTRASTS, patches_dev, model_width)
    recv_ids = (
        got[:, token_len:].reshape(cycle_size, id_width)[:, :per_peer]
        .astype(jnp.int32)
        .reshape(CONTRASTS, 1, patches_dev)
    )
    patch_iota = lax.broadcasted_iota(jnp.int32, (CONTRASTS, patches_dev, patches_dev), 1)
    selector = (recv_ids == patch_iota).astype(jnp.bfloat16)
    arranged = jnp.einsum(
        "cpk,ckd->cpd", selector, recv_rows, preferred_element_type=jnp.float32
    )
    joined = jnp.sum(arranged * contrast_gain.astype(jnp.float32)[:, None, :], axis=0)

    inverse_rms = lax.rsqrt(jnp.mean(joined * joined, axis=-1, keepdims=True) + 1e-05)
    normed = (joined * inverse_rms * norm_gain.astype(jnp.float32)).astype(jnp.bfloat16)
    pair_weight = jnp.concatenate(
        [
            w_key.reshape(model_width, head_count, head_width),
            w_value.reshape(model_width, head_count, head_width),
        ],
        axis=-1,
    )
    pair_rows = jnp.einsum(
        "pf,fhe->hpe", normed, pair_weight, preferred_element_type=jnp.float32
    ).astype(jnp.bfloat16)
    query_parts = jnp.transpose(queries.reshape(lat_rows, head_count, head_width), (1, 0, 2))
    query_parts = query_parts.reshape(head_count, -1, 2 * head_width)
    query_len = query_parts.shape[1]
    pair_payload = jnp.tile(jnp.concatenate([pair_rows, query_parts], axis=1), (copies, 1, 1))
    got_pairs = lax.all_to_all(pair_payload, "blk", split_axis=0, concat_axis=0, tiled=True)
    head_queries = lax.dynamic_slice_in_dim(
        got_pairs[:, patches_dev:], group_start, head_count, axis=0
    ).reshape(head_count * lat_rows, head_width)
    got_pairs = got_pairs[:, :patches_dev].reshape(cycle_size * patches_dev, 2 * head_width)
    head_keys = got_pairs[:, :head_width]
    head_values = got_pairs[:, head_width:]

    scores = jnp.einsum(
        "ld,kd->lk", head_queries, head_keys, preferred_element_type=jnp.float32
    )
    maxima = jnp.max(scores, axis=-1, keepdims=True)
    weights = jnp.exp(scores - maxima)
    totals = jnp.sum(weights, axis=-1, keepdims=True)
    summed = jnp.dot(weights.astype(jnp.bfloat16), head_values, preferred_element_type=jnp.float32)
    attended_head = (summed / totals).astype(jnp.bfloat16).reshape(head_count, lat_rows, head_width)
    got_attended = lax.all_to_all(
        jnp.tile(attended_head, (copies, 1, 1)), "blk", split_axis=0, concat_axis=0, tiled=True
    )
    attended = jnp.transpose(
        lax.dynamic_slice_in_dim(got_attended, group_start, head_count, axis=0), (1, 0, 2)
    ).reshape(lat_rows, model_width)
    mixed = latents.astype(jnp.float32) + jnp.dot(
        attended, w_out, preferred_element_type=jnp.float32
    )
    return mixed.astype(jnp.bfloat16)


def solution(mesh):
    in_specs = (
        P(("grp", "blk"), None),
        P(("grp", "blk")),
        P("blk", None),
        P(),
        P(),
        P(),
        P(),
        P(),
        P(),
    )
    out_specs = P(("grp", "blk"), None)
    return jax.shard_map(local, mesh=mesh, in_specs=in_specs, out_specs=out_specs, check_vma=False)
```

```python
import jax
import jax.numpy as jnp
from jax import lax
from jax.sharding import PartitionSpec as P

HEADS = 16
CONTRASTS = 4


def local(tokens, patch_of_row, latents, contrast_gain, norm_gain, w_query, w_key, w_value, w_out):
    cycle_size = lax.axis_size("blk")
    my_index = lax.axis_index("blk")
    tok_rows, model_width = tokens.shape
    head_count = HEADS
    head_width = model_width // head_count
    lat_rows = latents.shape[0]
    copies = cycle_size // head_count
    group_start = (my_index // head_count) * head_count
    per_peer = tok_rows // cycle_size
    patches_dev = tok_rows // CONTRASTS
    lanes = 128

    queries = (
        jnp.dot(latents, w_query, preferred_element_type=jnp.float32) * head_width ** (-0.5)
    ).astype(jnp.bfloat16)
    token_parts = jnp.transpose(
        tokens.reshape(per_peer, cycle_size, model_width), (1, 0, 2)
    ).reshape(cycle_size, -1, lanes)
    row_dest = lax.broadcasted_iota(jnp.int32, (tok_rows,), 0) % cycle_size
    local_ids = (patch_of_row - row_dest * patches_dev).astype(jnp.bfloat16)
    id_parts = jnp.transpose(local_ids.reshape(per_peer, cycle_size))
    id_width = -(-per_peer // lanes) * lanes
    id_parts = jnp.pad(id_parts, ((0, 0), (0, id_width - per_peer))).reshape(cycle_size, -1, lanes)
    token_len = token_parts.shape[1]
    payload = jnp.concatenate([token_parts, id_parts], axis=1)
    got = lax.all_to_all(payload, "blk", split_axis=0, concat_axis=0, tiled=True)

    recv_rows = got[:, :token_len].reshape(CONTRASTS, patches_dev, model_width)
    recv_ids = (
        got[:, token_len:].reshape(cycle_size, id_width)[:, :per_peer]
        .astype(jnp.int32)
        .reshape(CONTRASTS, 1, patches_dev)
    )
    patch_iota = lax.broadcasted_iota(jnp.int32, (CONTRASTS, patches_dev, patches_dev), 1)
    selector = (recv_ids == patch_iota).astype(jnp.bfloat16)
    arranged = jnp.einsum(
        "cpk,ckd->cpd", selector, recv_rows, preferred_element_type=jnp.float32
    )
    joined = jnp.sum(arranged * contrast_gain.astype(jnp.float32)[:, None, :], axis=0)

    inverse_rms = lax.rsqrt(jnp.mean(joined * joined, axis=-1, keepdims=True) + 1e-05)
    normed = (joined * inverse_rms * norm_gain.astype(jnp.float32)).astype(jnp.bfloat16)
    pair_weight = jnp.concatenate(
        [
            w_key.reshape(model_width, head_count, head_width),
            w_value.reshape(model_width, head_count, head_width),
        ],
        axis=-1,
    )
    pair_rows = jnp.dot(
        normed,
        pair_weight.reshape(model_width, 2 * model_width),
        preferred_element_type=jnp.float32,
    ).astype(jnp.bfloat16)
    pair_rows = jnp.transpose(pair_rows.reshape(patches_dev, head_count, 2 * head_width), (1, 0, 2))
    query_parts = jnp.transpose(queries.reshape(lat_rows, head_count, head_width), (1, 0, 2))
    query_parts = query_parts.reshape(head_count, -1, 2 * head_width)
    query_len = query_parts.shape[1]
    pair_payload = jnp.tile(jnp.concatenate([pair_rows, query_parts], axis=1), (copies, 1, 1))
    got_pairs = lax.all_to_all(pair_payload, "blk", split_axis=0, concat_axis=0, tiled=True)
    head_queries = lax.dynamic_slice_in_dim(
        got_pairs[:, patches_dev:], group_start, head_count, axis=0
    ).reshape(head_count * lat_rows, head_width)
    got_pairs = got_pairs[:, :patches_dev].reshape(cycle_size * patches_dev, 2 * head_width)
    head_keys = got_pairs[:, :head_width]
    head_values = got_pairs[:, head_width:]

    scores = jnp.einsum(
        "ld,kd->lk", head_queries, head_keys, preferred_element_type=jnp.float32
    )
    maxima = jnp.max(scores, axis=-1, keepdims=True)
    weights = jnp.exp(scores - maxima)
    totals = jnp.sum(weights, axis=-1, keepdims=True)
    summed = jnp.dot(weights.astype(jnp.bfloat16), head_values, preferred_element_type=jnp.float32)
    attended_head = (summed / totals).astype(jnp.bfloat16).reshape(head_count, lat_rows, head_width)
    got_attended = lax.all_to_all(
        jnp.tile(attended_head, (copies, 1, 1)), "blk", split_axis=0, concat_axis=0, tiled=True
    )
    attended = jnp.transpose(
        lax.dynamic_slice_in_dim(got_attended, group_start, head_count, axis=0), (1, 0, 2)
    ).reshape(lat_rows, model_width)
    mixed = latents.astype(jnp.float32) + jnp.dot(
        attended, w_out, preferred_element_type=jnp.float32
    )
    return mixed.astype(jnp.bfloat16)


def solution(mesh):
    in_specs = (
        P(("grp", "blk"), None),
        P(("grp", "blk")),
        P("blk", None),
        P(),
        P(),
        P(),
        P(),
        P(),
        P(),
    )
    out_specs = P(("grp", "blk"), None)
    return jax.shard_map(local, mesh=mesh, in_specs=in_specs, out_specs=out_specs, check_vma=False)
```

```python
import jax
import jax.numpy as jnp
from jax import lax
from jax.sharding import PartitionSpec as P

HEADS = 16
CONTRASTS = 4


def local(tokens, patch_of_row, latents, contrast_gain, norm_gain, w_query, w_key, w_value, w_out):
    cycle_size = lax.axis_size("blk")
    my_index = lax.axis_index("blk")
    tok_rows, model_width = tokens.shape
    head_count = HEADS
    head_width = model_width // head_count
    lat_rows = latents.shape[0]
    copies = cycle_size // head_count
    group_start = (my_index // head_count) * head_count
    per_peer = tok_rows // cycle_size
    patches_dev = tok_rows // CONTRASTS
    lanes = 128

    queries = (
        jnp.dot(latents, w_query, preferred_element_type=jnp.float32) * head_width ** (-0.5)
    ).astype(jnp.bfloat16)
    row_dest = lax.broadcasted_iota(jnp.int32, (tok_rows,), 0) % cycle_size
    local_ids = (patch_of_row - row_dest * patches_dev).astype(jnp.bfloat16)
    id_lanes = jnp.pad(local_ids[:, None], ((0, 0), (0, lanes - 1)))
    payload = jnp.transpose(
        jnp.concatenate([tokens, id_lanes], axis=1).reshape(
            per_peer, cycle_size, model_width + lanes
        ),
        (1, 0, 2),
    )
    got = lax.all_to_all(payload, "blk", split_axis=0, concat_axis=0, tiled=True)

    recv_rows = got[:, :, :model_width].reshape(CONTRASTS, patches_dev, model_width)
    recv_ids = got[:, :, model_width].astype(jnp.int32).reshape(CONTRASTS, 1, patches_dev)
    patch_iota = lax.broadcasted_iota(jnp.int32, (CONTRASTS, patches_dev, patches_dev), 1)
    selector = (recv_ids == patch_iota).astype(jnp.bfloat16)
    arranged = jnp.einsum(
        "cpk,ckd->cpd", selector, recv_rows, preferred_element_type=jnp.float32
    )
    joined = jnp.sum(arranged * contrast_gain.astype(jnp.float32)[:, None, :], axis=0)

    inverse_rms = lax.rsqrt(jnp.mean(joined * joined, axis=-1, keepdims=True) + 1e-05)
    normed = (joined * inverse_rms * norm_gain.astype(jnp.float32)).astype(jnp.bfloat16)
    pair_weight = jnp.concatenate(
        [
            w_key.reshape(model_width, head_count, head_width),
            w_value.reshape(model_width, head_count, head_width),
        ],
        axis=-1,
    )
    pair_rows = jnp.dot(
        normed,
        pair_weight.reshape(model_width, 2 * model_width),
        preferred_element_type=jnp.float32,
    ).astype(jnp.bfloat16)
    pair_rows = jnp.transpose(pair_rows.reshape(patches_dev, head_count, 2 * head_width), (1, 0, 2))
    query_parts = jnp.transpose(queries.reshape(lat_rows, head_count, head_width), (1, 0, 2))
    query_parts = query_parts.reshape(head_count, -1, 2 * head_width)
    query_len = query_parts.shape[1]
    pair_payload = jnp.tile(jnp.concatenate([pair_rows, query_parts], axis=1), (copies, 1, 1))
    got_pairs = lax.all_to_all(pair_payload, "blk", split_axis=0, concat_axis=0, tiled=True)
    head_queries = lax.dynamic_slice_in_dim(
        got_pairs[:, patches_dev:], group_start, head_count, axis=0
    ).reshape(head_count * lat_rows, head_width)
    got_pairs = got_pairs[:, :patches_dev].reshape(cycle_size * patches_dev, 2 * head_width)
    head_keys = got_pairs[:, :head_width]
    head_values = got_pairs[:, head_width:]

    scores = jnp.einsum(
        "ld,kd->lk", head_queries, head_keys, preferred_element_type=jnp.float32
    )
    maxima = jnp.max(scores, axis=-1, keepdims=True)
    weights = jnp.exp(scores - maxima)
    totals = jnp.sum(weights, axis=-1, keepdims=True)
    summed = jnp.dot(weights.astype(jnp.bfloat16), head_values, preferred_element_type=jnp.float32)
    attended_head = (summed / totals).astype(jnp.bfloat16).reshape(head_count, lat_rows, head_width)
    got_attended = lax.all_to_all(
        jnp.tile(attended_head, (copies, 1, 1)), "blk", split_axis=0, concat_axis=0, tiled=True
    )
    attended = jnp.transpose(
        lax.dynamic_slice_in_dim(got_attended, group_start, head_count, axis=0), (1, 0, 2)
    ).reshape(lat_rows, model_width)
    mixed = latents.astype(jnp.float32) + jnp.dot(
        attended, w_out, preferred_element_type=jnp.float32
    )
    return mixed.astype(jnp.bfloat16)


def solution(mesh):
    in_specs = (
        P(("grp", "blk"), None),
        P(("grp", "blk")),
        P("blk", None),
        P(),
        P(),
        P(),
        P(),
        P(),
        P(),
    )
    out_specs = P(("grp", "blk"), None)
    return jax.shard_map(local, mesh=mesh, in_specs=in_specs, out_specs=out_specs, check_vma=False)
```

```python
import jax
import jax.numpy as jnp
from jax import lax
from jax.sharding import Mesh
from jax.sharding import PartitionSpec as P

HEADS = 16
CONTRASTS = 4
SIDE = 8
BLK = ("side", "rest")


def split_exact(value, upward):
    high = value.astype(jnp.bfloat16)
    rest = value - high.astype(jnp.float32)
    if upward:
        rest = rest + jnp.abs(rest) * (2.0 ** -8)
    return high, rest.astype(jnp.bfloat16)


def local(tokens, patch_of_row, latents, contrast_gain, norm_gain, w_query, w_key, w_value, w_out):
    cycle_size = lax.axis_size(BLK)
    my_index = lax.axis_index(BLK)
    side_size = lax.axis_size("rest")
    sides = cycle_size // side_size
    tok_rows, model_width = tokens.shape
    head_count = HEADS
    head_width = model_width // head_count
    heads_dev = head_count // side_size
    pair_width = heads_dev * head_width
    lat_rows = latents.shape[0]
    all_lat = lat_rows * cycle_size
    per_peer = tok_rows // cycle_size
    patches_dev = tok_rows // CONTRASTS
    lanes = 128
    query_lanes = (lat_rows * pair_width) // per_peer

    queries = (
        jnp.dot(latents, w_query, preferred_element_type=jnp.float32) * head_width ** (-0.5)
    ).astype(jnp.bfloat16)
    query_parts = jnp.tile(
        jnp.transpose(queries.reshape(lat_rows, side_size, pair_width), (1, 0, 2)),
        (sides, 1, 1),
    )
    embed = query_lanes < lanes
    if not embed:
        query_lanes = 0
    row_dest = lax.broadcasted_iota(jnp.int32, (tok_rows,), 0) % cycle_size
    local_ids = (patch_of_row - row_dest * patches_dev).astype(jnp.bfloat16)
    id_lanes = jnp.pad(local_ids[:, None], ((0, 0), (0, lanes - query_lanes - 1)))
    payload = jnp.transpose(
        jnp.concatenate([tokens, id_lanes], axis=1).reshape(
            per_peer, cycle_size, model_width + lanes - query_lanes
        ),
        (1, 0, 2),
    )
    if embed:
        payload = jnp.concatenate(
            [payload, query_parts.reshape(cycle_size, per_peer, query_lanes)], axis=2
        )
        got = lax.all_to_all(payload, BLK, split_axis=0, concat_axis=0, tiled=True)
        got_queries = got[:, :, model_width + lanes - query_lanes :]
    else:
        got = lax.all_to_all(payload, BLK, split_axis=0, concat_axis=0, tiled=True)
        got_queries = lax.all_to_all(query_parts, BLK, split_axis=0, concat_axis=0, tiled=True)

    recv_rows = got[:, :, :model_width].reshape(CONTRASTS, patches_dev, model_width)
    recv_ids = got[:, :, model_width].astype(jnp.int32).reshape(CONTRASTS, 1, patches_dev)
    head_queries = jnp.transpose(
        got_queries.reshape(all_lat, heads_dev, head_width), (1, 0, 2)
    )
    patch_iota = lax.broadcasted_iota(jnp.int32, (CONTRASTS, patches_dev, patches_dev), 1)
    selector = (recv_ids == patch_iota).astype(jnp.bfloat16)
    arranged = jnp.einsum(
        "cpk,ckd->cpd", selector, recv_rows, preferred_element_type=jnp.float32
    )
    joined = jnp.sum(arranged * contrast_gain.astype(jnp.float32)[:, None, :], axis=0)

    inverse_rms = lax.rsqrt(jnp.mean(joined * joined, axis=-1, keepdims=True) + 1e-05)
    normed = (joined * inverse_rms * norm_gain.astype(jnp.float32)).astype(jnp.bfloat16)
    pair_weight = jnp.concatenate(
        [
            w_key.reshape(model_width, head_count, head_width),
            w_value.reshape(model_width, head_count, head_width),
        ],
        axis=-1,
    )
    pair_rows = jnp.dot(
        normed,
        pair_weight.reshape(model_width, 2 * model_width),
        preferred_element_type=jnp.float32,
    ).astype(jnp.bfloat16)
    pair_rows = jnp.transpose(
        pair_rows.reshape(patches_dev, side_size, 2 * pair_width), (1, 0, 2)
    )
    got_pairs = lax.all_to_all(pair_rows, "rest", split_axis=0, concat_axis=0, tiled=True)
    got_pairs = jnp.transpose(
        got_pairs.reshape(side_size * patches_dev, heads_dev, 2 * head_width), (1, 0, 2)
    )
    head_keys = got_pairs[:, :, :head_width]
    head_values = got_pairs[:, :, head_width:]

    scores = jnp.einsum(
        "hld,hkd->hlk", head_queries, head_keys, preferred_element_type=jnp.float32
    )
    maxima = jnp.max(scores, axis=-1)
    max_high, max_low = split_exact(maxima, True)
    shift = max_high.astype(jnp.float32) + max_low.astype(jnp.float32)
    weights = jnp.exp(scores - shift[..., None])
    totals = jnp.sum(weights, axis=-1)
    tot_high, tot_low = split_exact(totals, False)
    summed = jnp.einsum(
        "hlk,hkd->lhd", weights.astype(jnp.bfloat16), head_values, preferred_element_type=jnp.float32
    ).astype(jnp.bfloat16)
    stats = jnp.transpose(jnp.stack([max_high, max_low, tot_high, tot_low], axis=-1), (1, 0, 2))
    part_payload = jnp.concatenate(
        [summed.reshape(all_lat, pair_width), stats.reshape(all_lat, heads_dev * 4)], axis=1
    ).reshape(cycle_size, lat_rows, pair_width + heads_dev * 4)
    got_parts = lax.all_to_all(part_payload, BLK, split_axis=0, concat_axis=0, tiled=True)
    got_parts = got_parts.astype(jnp.float32).reshape(sides, side_size, lat_rows, -1)
    part_sums = got_parts[..., :pair_width].reshape(
        sides, side_size, lat_rows, heads_dev, head_width
    )
    part_stats = got_parts[..., pair_width:].reshape(sides, side_size, lat_rows, heads_dev, 4)
    part_max = part_stats[..., 0] + part_stats[..., 1]
    part_tot = part_stats[..., 2] + part_stats[..., 3]
    top = jnp.max(part_max, axis=0)
    factor = jnp.exp(part_max - top[None])
    total = jnp.sum(part_tot * factor, axis=0)
    accum = jnp.sum(part_sums * factor[..., None], axis=0)
    attended = (accum / total[..., None]).astype(jnp.bfloat16)
    attended = jnp.transpose(attended, (1, 0, 2, 3)).reshape(lat_rows, model_width)
    mixed = latents.astype(jnp.float32) + jnp.dot(
        attended, w_out, preferred_element_type=jnp.float32
    )
    return mixed.astype(jnp.bfloat16)


def solution(mesh):
    groups, blocks = mesh.devices.shape
    side_mesh = Mesh(
        mesh.devices.reshape(groups, blocks // SIDE, SIDE), ("grp",) + BLK
    )
    rows = ("grp",) + BLK
    in_specs = (
        P(rows, None),
        P(rows),
        P(BLK, None),
        P(),
        P(),
        P(),
        P(),
        P(),
        P(),
    )
    out_specs = P(rows, None)
    return jax.shard_map(
        local, mesh=side_mesh, in_specs=in_specs, out_specs=out_specs, check_vma=False
    )
```

```python
import jax
import jax.numpy as jnp
from jax import lax
from jax.sharding import Mesh
from jax.sharding import PartitionSpec as P

HEADS = 16
CONTRASTS = 4
SIDE = 8
BLK = ("side", "rest")


def split_exact(value, upward):
    high = value.astype(jnp.bfloat16)
    rest = value - high.astype(jnp.float32)
    if upward:
        rest = rest + jnp.abs(rest) * (2.0 ** -8)
    return high, rest.astype(jnp.bfloat16)


def local(tokens, patch_of_row, latents, contrast_gain, norm_gain, w_query, w_key, w_value, w_out):
    cycle_size = lax.axis_size(BLK)
    my_index = lax.axis_index(BLK)
    side_size = lax.axis_size("rest")
    sides = cycle_size // side_size
    tok_rows, model_width = tokens.shape
    head_count = HEADS
    head_width = model_width // head_count
    heads_dev = head_count // side_size
    pair_width = heads_dev * head_width
    lat_rows = latents.shape[0]
    all_lat = lat_rows * cycle_size
    per_peer = tok_rows // cycle_size
    patches_dev = tok_rows // CONTRASTS
    lanes = 128
    query_lanes = (lat_rows * pair_width) // per_peer

    queries = (
        jnp.dot(latents, w_query, preferred_element_type=jnp.float32) * head_width ** (-0.5)
    ).astype(jnp.bfloat16)
    query_parts = jnp.tile(
        jnp.transpose(queries.reshape(lat_rows, side_size, pair_width), (1, 0, 2)),
        (sides, 1, 1),
    )
    embed = query_lanes < lanes
    if not embed:
        query_lanes = 0
    row_dest = lax.broadcasted_iota(jnp.int32, (tok_rows,), 0) % cycle_size
    local_ids = (patch_of_row - row_dest * patches_dev).astype(jnp.bfloat16)
    id_lanes = jnp.pad(local_ids[:, None], ((0, 0), (0, lanes - query_lanes - 1)))
    payload = jnp.transpose(
        jnp.concatenate([tokens, id_lanes], axis=1).reshape(
            per_peer, cycle_size, model_width + lanes - query_lanes
        ),
        (1, 0, 2),
    )
    if embed:
        payload = jnp.concatenate(
            [payload, query_parts.reshape(cycle_size, per_peer, query_lanes)], axis=2
        )
        got = lax.all_to_all(payload, BLK, split_axis=0, concat_axis=0, tiled=True)
        got_queries = got[:, :, model_width + lanes - query_lanes :]
    else:
        got = lax.all_to_all(payload, BLK, split_axis=0, concat_axis=0, tiled=True)
        got_queries = lax.all_to_all(query_parts, BLK, split_axis=0, concat_axis=0, tiled=True)

    recv_rows = got[:, :, :model_width].reshape(CONTRASTS, patches_dev, model_width)
    recv_ids = got[:, :, model_width].astype(jnp.int32).reshape(CONTRASTS, 1, patches_dev)
    head_queries = jnp.transpose(
        got_queries.reshape(all_lat, heads_dev, head_width), (1, 0, 2)
    )
    patch_iota = lax.broadcasted_iota(jnp.int32, (CONTRASTS, patches_dev, patches_dev), 1)
    selector = (recv_ids == patch_iota).astype(jnp.bfloat16)
    arranged = jnp.einsum(
        "cpk,ckd->cpd", selector, recv_rows, preferred_element_type=jnp.float32
    )
    joined = jnp.sum(arranged * contrast_gain.astype(jnp.float32)[:, None, :], axis=0)

    inverse_rms = lax.rsqrt(jnp.mean(joined * joined, axis=-1, keepdims=True) + 1e-05)
    normed = (joined * inverse_rms * norm_gain.astype(jnp.float32)).astype(jnp.bfloat16)
    pair_weight = jnp.concatenate(
        [
            w_key.reshape(model_width, head_count, head_width),
            w_value.reshape(model_width, head_count, head_width),
        ],
        axis=-1,
    )
    pair_rows = jnp.dot(
        normed,
        pair_weight.reshape(model_width, 2 * model_width),
        preferred_element_type=jnp.float32,
    ).astype(jnp.bfloat16)
    pair_rows = jnp.transpose(
        pair_rows.reshape(patches_dev, side_size, 2 * pair_width), (1, 0, 2)
    )
    got_pairs = lax.all_to_all(pair_rows, "rest", split_axis=0, concat_axis=0, tiled=True)
    got_pairs = jnp.transpose(
        got_pairs.reshape(side_size * patches_dev, heads_dev, 2 * head_width), (1, 0, 2)
    )
    head_keys = got_pairs[:, :, :head_width]
    head_values = got_pairs[:, :, head_width:]

    scores = jnp.einsum(
        "hld,hkd->hlk", head_queries, head_keys, preferred_element_type=jnp.float32
    )
    maxima = jnp.max(scores, axis=-1)
    max_high, max_low = split_exact(maxima, True)
    shift = max_high.astype(jnp.float32) + max_low.astype(jnp.float32)
    weights = jnp.exp(scores - shift[..., None])
    totals = jnp.sum(weights, axis=-1)
    tot_high, tot_low = split_exact(totals, False)
    summed = jnp.einsum(
        "hlk,hkd->lhd", weights.astype(jnp.bfloat16), head_values, preferred_element_type=jnp.float32
    ).astype(jnp.bfloat16)
    stats = jnp.transpose(jnp.stack([max_high, max_low, tot_high, tot_low], axis=-1), (1, 0, 2))
    part_payload = jnp.concatenate(
        [
            summed.reshape(cycle_size, lat_rows * pair_width),
            stats.reshape(cycle_size, lat_rows * heads_dev * 4),
        ],
        axis=1,
    ).reshape(cycle_size, 1, -1)
    got_parts = lax.all_to_all(part_payload, BLK, split_axis=0, concat_axis=0, tiled=True)
    got_parts = got_parts.astype(jnp.float32).reshape(sides, side_size, -1)
    part_sums = got_parts[..., : lat_rows * pair_width].reshape(
        sides, side_size, lat_rows, heads_dev, head_width
    )
    part_stats = got_parts[..., lat_rows * pair_width :].reshape(
        sides, side_size, lat_rows, heads_dev, 4
    )
    part_max = part_stats[..., 0] + part_stats[..., 1]
    part_tot = part_stats[..., 2] + part_stats[..., 3]
    top = jnp.max(part_max, axis=0)
    factor = jnp.exp(part_max - top[None])
    total = jnp.sum(part_tot * factor, axis=0)
    accum = jnp.sum(part_sums * factor[..., None], axis=0)
    attended = (accum / total[..., None]).astype(jnp.bfloat16)
    attended = jnp.transpose(attended, (1, 0, 2, 3)).reshape(lat_rows, model_width)
    mixed = latents.astype(jnp.float32) + jnp.dot(
        attended, w_out, preferred_element_type=jnp.float32
    )
    return mixed.astype(jnp.bfloat16)


def solution(mesh):
    groups, blocks = mesh.devices.shape
    side_mesh = Mesh(
        mesh.devices.reshape(groups, blocks // SIDE, SIDE), ("grp",) + BLK
    )
    rows = ("grp",) + BLK
    in_specs = (
        P(rows, None),
        P(rows),
        P(BLK, None),
        P(),
        P(),
        P(),
        P(),
        P(),
        P(),
    )
    out_specs = P(rows, None)
    return jax.shard_map(
        local, mesh=side_mesh, in_specs=in_specs, out_specs=out_specs, check_vma=False
    )
```

```python
import jax
import jax.numpy as jnp
from jax import lax
from jax.sharding import Mesh
from jax.sharding import PartitionSpec as P

HEADS = 16
CONTRASTS = 4
SIDE = 8
BLK = ("side", "rest")


def split_exact(value, upward):
    high = value.astype(jnp.bfloat16)
    rest = value - high.astype(jnp.float32)
    if upward:
        rest = rest + jnp.abs(rest) * (2.0 ** -8)
    return high, rest.astype(jnp.bfloat16)


def local(tokens, patch_of_row, latents, contrast_gain, norm_gain, w_query, w_key, w_value, w_out):
    cycle_size = lax.axis_size(BLK)
    my_index = lax.axis_index(BLK)
    side_size = lax.axis_size("rest")
    sides = cycle_size // side_size
    tok_rows, model_width = tokens.shape
    head_count = HEADS
    head_width = model_width // head_count
    heads_dev = head_count // side_size
    pair_width = heads_dev * head_width
    lat_rows = latents.shape[0]
    all_lat = lat_rows * cycle_size
    per_peer = tok_rows // cycle_size
    patches_dev = tok_rows // CONTRASTS
    lanes = 128
    query_lanes = (lat_rows * pair_width) // per_peer

    queries = (
        jnp.dot(latents, w_query, preferred_element_type=jnp.float32) * head_width ** (-0.5)
    ).astype(jnp.bfloat16)
    query_parts = jnp.tile(
        jnp.transpose(queries.reshape(lat_rows, side_size, pair_width), (1, 0, 2)),
        (sides, 1, 1),
    )
    embed = query_lanes < lanes
    if not embed:
        query_lanes = 0
    row_dest = lax.broadcasted_iota(jnp.int32, (tok_rows,), 0) % cycle_size
    local_ids = (patch_of_row - row_dest * patches_dev).astype(jnp.bfloat16)
    id_lanes = jnp.pad(local_ids[:, None], ((0, 0), (0, lanes - query_lanes - 1)))
    payload = jnp.transpose(
        jnp.concatenate([tokens, id_lanes], axis=1).reshape(
            per_peer, cycle_size, model_width + lanes - query_lanes
        ),
        (1, 0, 2),
    )
    if embed:
        payload = jnp.concatenate(
            [payload, query_parts.reshape(cycle_size, per_peer, query_lanes)], axis=2
        )
        got = lax.all_to_all(payload, BLK, split_axis=0, concat_axis=0, tiled=True)
        got_queries = got[:, :, model_width + lanes - query_lanes :]
    else:
        got = lax.all_to_all(payload, BLK, split_axis=0, concat_axis=0, tiled=True)
        got_queries = lax.all_to_all(query_parts, BLK, split_axis=0, concat_axis=0, tiled=True)

    recv_rows = got[:, :, :model_width].reshape(CONTRASTS, patches_dev, model_width)
    recv_ids = got[:, :, model_width].astype(jnp.int32).reshape(CONTRASTS, 1, patches_dev)
    head_queries = jnp.transpose(
        got_queries.reshape(all_lat, heads_dev, head_width), (1, 0, 2)
    )
    patch_iota = lax.broadcasted_iota(jnp.int32, (CONTRASTS, patches_dev, patches_dev), 1)
    selector = (recv_ids == patch_iota).astype(jnp.bfloat16)
    arranged = jnp.einsum(
        "cpk,ckd->cpd", selector, recv_rows, preferred_element_type=jnp.float32
    )
    joined = jnp.sum(arranged * contrast_gain.astype(jnp.float32)[:, None, :], axis=0)

    inverse_rms = lax.rsqrt(jnp.mean(joined * joined, axis=-1, keepdims=True) + 1e-05)
    normed = (joined * inverse_rms * norm_gain.astype(jnp.float32)).astype(jnp.bfloat16)
    pair_weight = jnp.concatenate(
        [
            w_key.reshape(model_width, head_count, head_width),
            w_value.reshape(model_width, head_count, head_width),
        ],
        axis=-1,
    )
    pair_rows = jnp.dot(
        normed,
        pair_weight.reshape(model_width, 2 * model_width),
        preferred_element_type=jnp.float32,
    ).astype(jnp.bfloat16)
    pair_rows = jnp.transpose(
        pair_rows.reshape(patches_dev, side_size, heads_dev, 2 * head_width), (1, 2, 0, 3)
    )
    got_pairs = lax.all_to_all(pair_rows, "rest", split_axis=0, concat_axis=2, tiled=True)
    got_pairs = got_pairs.reshape(heads_dev, side_size * patches_dev, 2 * head_width)
    head_keys = got_pairs[:, :, :head_width]
    head_values = got_pairs[:, :, head_width:]

    scores = jnp.einsum(
        "hld,hkd->hlk", head_queries, head_keys, preferred_element_type=jnp.float32
    )
    maxima = jnp.max(scores, axis=-1)
    max_high, max_low = split_exact(maxima, True)
    shift = max_high.astype(jnp.float32) + max_low.astype(jnp.float32)
    weights = jnp.exp(scores - shift[..., None])
    totals = jnp.sum(weights, axis=-1)
    tot_high, tot_low = split_exact(totals, False)
    summed = jnp.einsum(
        "hlk,hkd->lhd", weights.astype(jnp.bfloat16), head_values, preferred_element_type=jnp.float32
    ).astype(jnp.bfloat16)
    stats = jnp.transpose(jnp.stack([max_high, max_low, tot_high, tot_low], axis=-1), (1, 0, 2))
    part_payload = jnp.concatenate(
        [summed.reshape(all_lat, pair_width), stats.reshape(all_lat, heads_dev * 4)], axis=1
    ).reshape(cycle_size, lat_rows, pair_width + heads_dev * 4)
    got_parts = lax.all_to_all(part_payload, BLK, split_axis=0, concat_axis=0, tiled=True)
    got_parts = got_parts.astype(jnp.float32).reshape(sides, side_size, lat_rows, -1)
    part_sums = got_parts[..., :pair_width].reshape(
        sides, side_size, lat_rows, heads_dev, head_width
    )
    part_stats = got_parts[..., pair_width:].reshape(sides, side_size, lat_rows, heads_dev, 4)
    part_max = part_stats[..., 0] + part_stats[..., 1]
    part_tot = part_stats[..., 2] + part_stats[..., 3]
    top = jnp.max(part_max, axis=0)
    factor = jnp.exp(part_max - top[None])
    total = jnp.sum(part_tot * factor, axis=0)
    accum = jnp.sum(part_sums * factor[..., None], axis=0)
    attended = (accum / total[..., None]).astype(jnp.bfloat16)
    attended = jnp.transpose(attended, (1, 0, 2, 3)).reshape(lat_rows, model_width)
    mixed = latents.astype(jnp.float32) + jnp.dot(
        attended, w_out, preferred_element_type=jnp.float32
    )
    return mixed.astype(jnp.bfloat16)


def solution(mesh):
    groups, blocks = mesh.devices.shape
    side_mesh = Mesh(
        mesh.devices.reshape(groups, blocks // SIDE, SIDE), ("grp",) + BLK
    )
    rows = ("grp",) + BLK
    in_specs = (
        P(rows, None),
        P(rows),
        P(BLK, None),
        P(),
        P(),
        P(),
        P(),
        P(),
        P(),
    )
    out_specs = P(rows, None)
    return jax.shard_map(
        local, mesh=side_mesh, in_specs=in_specs, out_specs=out_specs, check_vma=False
    )
```

```python
import jax
import jax.numpy as jnp
from jax import lax
from jax.sharding import PartitionSpec as P

HEADS = 16
CONTRASTS = 4


def shifted(block, axis, distance):
    size = lax.axis_size(axis)
    return lax.ppermute(block, axis, [(i, (i + distance) % size) for i in range(size)])


def local(tokens, patch_of_row, latents, contrast_gain, norm_gain, w_query, w_key, w_value, w_out):
    cycle_size = lax.axis_size("blk")
    my_index = lax.axis_index("blk")
    tok_rows, model_width = tokens.shape
    head_count = HEADS
    head_width = model_width // head_count
    lat_rows = latents.shape[0]
    copies = cycle_size // head_count
    group_start = (my_index // head_count) * head_count
    per_peer = tok_rows // cycle_size
    patches_dev = tok_rows // CONTRASTS
    lanes = 128

    queries = (
        jnp.dot(latents, w_query, preferred_element_type=jnp.float32) * head_width ** (-0.5)
    ).astype(jnp.bfloat16)
    row_dest = lax.broadcasted_iota(jnp.int32, (tok_rows,), 0) % cycle_size
    local_ids = (patch_of_row - row_dest * patches_dev).astype(jnp.bfloat16)
    id_lanes = jnp.pad(local_ids[:, None], ((0, 0), (0, lanes - 1)))
    payload = jnp.transpose(
        jnp.concatenate([tokens, id_lanes], axis=1).reshape(
            per_peer, cycle_size, model_width + lanes
        ),
        (1, 0, 2),
    )
    got = lax.all_to_all(payload, "blk", split_axis=0, concat_axis=0, tiled=True)

    recv_rows = got[:, :, :model_width].reshape(CONTRASTS, patches_dev, model_width)
    recv_ids = got[:, :, model_width].astype(jnp.int32).reshape(CONTRASTS, 1, patches_dev)
    patch_iota = lax.broadcasted_iota(jnp.int32, (CONTRASTS, patches_dev, patches_dev), 1)
    selector = (recv_ids == patch_iota).astype(jnp.bfloat16)
    arranged = jnp.einsum(
        "cpk,ckd->cpd", selector, recv_rows, preferred_element_type=jnp.float32
    )
    joined = jnp.sum(arranged * contrast_gain.astype(jnp.float32)[:, None, :], axis=0)

    inverse_rms = lax.rsqrt(jnp.mean(joined * joined, axis=-1, keepdims=True) + 1e-05)
    normed = (joined * inverse_rms * norm_gain.astype(jnp.float32)).astype(jnp.bfloat16)
    pair_weight = jnp.concatenate(
        [
            w_key.reshape(model_width, head_count, head_width),
            w_value.reshape(model_width, head_count, head_width),
        ],
        axis=-1,
    )
    pair_rows = jnp.dot(
        normed,
        pair_weight.reshape(model_width, 2 * model_width),
        preferred_element_type=jnp.float32,
    ).astype(jnp.bfloat16)
    pair_rows = jnp.transpose(pair_rows.reshape(patches_dev, head_count, 2 * head_width), (1, 0, 2))
    query_parts = jnp.transpose(queries.reshape(lat_rows, head_count, head_width), (1, 0, 2))
    query_parts = query_parts.reshape(head_count, -1, 2 * head_width)
    query_len = query_parts.shape[1]
    pair_payload = jnp.tile(jnp.concatenate([pair_rows, query_parts], axis=1), (copies, 1, 1))
    if copies == 1:
        blocks = [pair_payload[my_index]]
        for step in range(1, cycle_size):
            sent = lax.dynamic_index_in_dim(
                pair_payload, (my_index + step) % cycle_size, axis=0, keepdims=False
            )
            blocks.append(shifted(sent, "blk", step))
        got_pairs = jnp.stack(blocks)
        head_queries = got_pairs[:, patches_dev:].reshape(head_count * lat_rows, head_width)
    else:
        got_pairs = lax.all_to_all(pair_payload, "blk", split_axis=0, concat_axis=0, tiled=True)
        head_queries = lax.dynamic_slice_in_dim(
            got_pairs[:, patches_dev:], group_start, head_count, axis=0
        ).reshape(head_count * lat_rows, head_width)
    got_pairs = got_pairs[:, :patches_dev].reshape(cycle_size * patches_dev, 2 * head_width)
    head_keys = got_pairs[:, :head_width]
    head_values = got_pairs[:, head_width:]

    scores = jnp.einsum(
        "ld,kd->lk", head_queries, head_keys, preferred_element_type=jnp.float32
    )
    maxima = jnp.max(scores, axis=-1, keepdims=True)
    weights = jnp.exp(scores - maxima)
    totals = jnp.sum(weights, axis=-1, keepdims=True)
    summed = jnp.dot(weights.astype(jnp.bfloat16), head_values, preferred_element_type=jnp.float32)
    attended_head = (summed / totals).astype(jnp.bfloat16).reshape(head_count, lat_rows, head_width)
    if copies == 1:
        attended_head = jnp.take(attended_head, (my_index - lax.broadcasted_iota(jnp.int32, (cycle_size,), 0)) % cycle_size, axis=0)
    got_attended = lax.all_to_all(
        jnp.tile(attended_head, (copies, 1, 1)), "blk", split_axis=0, concat_axis=0, tiled=True
    )
    attended = jnp.transpose(
        lax.dynamic_slice_in_dim(got_attended, group_start, head_count, axis=0), (1, 0, 2)
    ).reshape(lat_rows, model_width)
    mixed = latents.astype(jnp.float32) + jnp.dot(
        attended, w_out, preferred_element_type=jnp.float32
    )
    return mixed.astype(jnp.bfloat16)


def solution(mesh):
    in_specs = (
        P(("grp", "blk"), None),
        P(("grp", "blk")),
        P("blk", None),
        P(),
        P(),
        P(),
        P(),
        P(),
        P(),
    )
    out_specs = P(("grp", "blk"), None)
    return jax.shard_map(local, mesh=mesh, in_specs=in_specs, out_specs=out_specs, check_vma=False)
```

```python
import jax
import jax.numpy as jnp
from jax import lax
from jax.sharding import Mesh
from jax.sharding import PartitionSpec as P

HEADS = 16
CONTRASTS = 4
SIDE = 8
BLK = ("side", "rest")


def split_exact(value, upward):
    high = value.astype(jnp.bfloat16)
    rest = value - high.astype(jnp.float32)
    if upward:
        rest = rest + jnp.abs(rest) * (2.0 ** -8)
    return high, rest.astype(jnp.bfloat16)


def local(tokens, patch_of_row, latents, contrast_gain, norm_gain, w_query, w_key, w_value, w_out):
    cycle_size = lax.axis_size(BLK)
    my_index = lax.axis_index(BLK)
    side_size = lax.axis_size("rest")
    sides = cycle_size // side_size
    tok_rows, model_width = tokens.shape
    head_count = HEADS
    head_width = model_width // head_count
    heads_dev = head_count // side_size
    pair_width = heads_dev * head_width
    lat_rows = latents.shape[0]
    all_lat = lat_rows * cycle_size
    per_peer = tok_rows // cycle_size
    patches_dev = tok_rows // CONTRASTS
    lanes = 128
    query_lanes = (lat_rows * pair_width) // per_peer

    queries = (
        jnp.dot(latents, w_query, preferred_element_type=jnp.float32) * head_width ** (-0.5)
    ).astype(jnp.bfloat16)
    query_parts = jnp.tile(
        jnp.transpose(queries.reshape(lat_rows, side_size, pair_width), (1, 0, 2)),
        (sides, 1, 1),
    )
    embed = query_lanes < lanes
    if not embed:
        query_lanes = 0
    row_dest = lax.broadcasted_iota(jnp.int32, (tok_rows,), 0) % cycle_size
    local_ids = (patch_of_row - row_dest * patches_dev).astype(jnp.bfloat16)
    id_lanes = jnp.pad(local_ids[:, None], ((0, 0), (0, lanes - query_lanes - 1)))
    payload = jnp.transpose(
        jnp.concatenate([tokens, id_lanes], axis=1).reshape(
            per_peer, cycle_size, model_width + lanes - query_lanes
        ),
        (1, 0, 2),
    )
    if embed:
        payload = jnp.concatenate(
            [payload, query_parts.reshape(cycle_size, per_peer, query_lanes)], axis=2
        )
        got = lax.all_to_all(payload, BLK, split_axis=0, concat_axis=0, tiled=True)
        got_queries = got[:, :, model_width + lanes - query_lanes :]
    else:
        got = lax.all_to_all(payload, BLK, split_axis=0, concat_axis=0, tiled=True)
        got_queries = lax.all_to_all(query_parts, BLK, split_axis=0, concat_axis=0, tiled=True)

    recv_rows = got[:, :, :model_width].reshape(CONTRASTS, patches_dev, model_width)
    recv_ids = got[:, :, model_width].astype(jnp.int32).reshape(CONTRASTS, 1, patches_dev)
    head_queries = jnp.transpose(
        got_queries.reshape(all_lat, heads_dev, head_width), (1, 0, 2)
    )
    patch_iota = lax.broadcasted_iota(jnp.int32, (CONTRASTS, patches_dev, patches_dev), 1)
    selector = (recv_ids == patch_iota).astype(jnp.bfloat16)
    arranged = jnp.einsum(
        "cpk,ckd->cpd", selector, recv_rows, preferred_element_type=jnp.float32
    )
    joined = jnp.sum(arranged * contrast_gain.astype(jnp.float32)[:, None, :], axis=0)

    inverse_rms = lax.rsqrt(jnp.mean(joined * joined, axis=-1, keepdims=True) + 1e-05)
    normed = (joined * inverse_rms * norm_gain.astype(jnp.float32)).astype(jnp.bfloat16)
    pair_weight = jnp.concatenate(
        [
            w_key.reshape(model_width, head_count, head_width),
            w_value.reshape(model_width, head_count, head_width),
        ],
        axis=-1,
    )
    pair_rows = jnp.dot(
        normed,
        pair_weight.reshape(model_width, 2 * model_width),
        preferred_element_type=jnp.float32,
    ).astype(jnp.bfloat16)
    pair_rows = jnp.transpose(
        pair_rows.reshape(patches_dev, side_size, 2 * pair_width), (1, 0, 2)
    )
    got_pairs = lax.all_to_all(pair_rows, "rest", split_axis=0, concat_axis=0, tiled=True)
    got_pairs = got_pairs.reshape(side_size * patches_dev, heads_dev * 2 * head_width)
    maxima, totals, summed = [], [], []
    for head in range(heads_dev):
        base = head * 2 * head_width
        scores = jnp.dot(
            head_queries[head],
            jnp.transpose(got_pairs[:, base : base + head_width]),
            preferred_element_type=jnp.float32,
        )
        head_max = jnp.max(scores, axis=-1)
        max_high, max_low = split_exact(head_max, True)
        shift = max_high.astype(jnp.float32) + max_low.astype(jnp.float32)
        weights = jnp.exp(scores - shift[:, None])
        head_tot = jnp.sum(weights, axis=-1)
        tot_high, tot_low = split_exact(head_tot, False)
        summed.append(
            jnp.dot(
                weights.astype(jnp.bfloat16),
                got_pairs[:, base + head_width : base + 2 * head_width],
                preferred_element_type=jnp.float32,
            ).astype(jnp.bfloat16)
        )
        maxima.append(jnp.stack([max_high, max_low, tot_high, tot_low], axis=-1))
    summed = jnp.stack(summed, axis=1)
    stats = jnp.stack(maxima, axis=1)
    part_payload = jnp.concatenate(
        [
            summed.reshape(cycle_size, lat_rows * pair_width),
            stats.reshape(cycle_size, lat_rows * heads_dev * 4),
        ],
        axis=1,
    ).reshape(cycle_size, 1, -1)
    got_parts = lax.all_to_all(part_payload, BLK, split_axis=0, concat_axis=0, tiled=True)
    got_parts = got_parts.astype(jnp.float32).reshape(sides, side_size, -1)
    part_sums = got_parts[..., : lat_rows * pair_width].reshape(
        sides, side_size, lat_rows, heads_dev, head_width
    )
    part_stats = got_parts[..., lat_rows * pair_width :].reshape(
        sides, side_size, lat_rows, heads_dev, 4
    )
    part_max = part_stats[..., 0] + part_stats[..., 1]
    part_tot = part_stats[..., 2] + part_stats[..., 3]
    top = jnp.max(part_max, axis=0)
    factor = jnp.exp(part_max - top[None])
    total = jnp.sum(part_tot * factor, axis=0)
    accum = jnp.sum(part_sums * factor[..., None], axis=0)
    attended = (accum / total[..., None]).astype(jnp.bfloat16)
    attended = jnp.transpose(attended, (1, 0, 2, 3)).reshape(lat_rows, model_width)
    mixed = latents.astype(jnp.float32) + jnp.dot(
        attended, w_out, preferred_element_type=jnp.float32
    )
    return mixed.astype(jnp.bfloat16)


def solution(mesh):
    groups, blocks = mesh.devices.shape
    side_mesh = Mesh(
        mesh.devices.reshape(groups, blocks // SIDE, SIDE), ("grp",) + BLK
    )
    rows = ("grp",) + BLK
    in_specs = (
        P(rows, None),
        P(rows),
        P(BLK, None),
        P(),
        P(),
        P(),
        P(),
        P(),
        P(),
    )
    out_specs = P(rows, None)
    return jax.shard_map(
        local, mesh=side_mesh, in_specs=in_specs, out_specs=out_specs, check_vma=False
    )
```

```python
import jax
import jax.numpy as jnp
from jax import lax
from jax.sharding import PartitionSpec as P

HEADS = 16
CONTRASTS = 4


def local(tokens, patch_of_row, latents, contrast_gain, norm_gain, w_query, w_key, w_value, w_out):
    cycle_size = lax.axis_size("blk")
    my_index = lax.axis_index("blk")
    tok_rows, model_width = tokens.shape
    head_count = HEADS
    head_width = model_width // head_count
    lat_rows = latents.shape[0]
    copies = cycle_size // head_count
    group_start = (my_index // head_count) * head_count
    per_peer = tok_rows // cycle_size
    patches_dev = tok_rows // CONTRASTS
    lanes = 128

    queries = (
        jnp.dot(latents, w_query, preferred_element_type=jnp.float32) * head_width ** (-0.5)
    ).astype(jnp.bfloat16)
    query_parts = jnp.tile(
        jnp.transpose(queries.reshape(lat_rows, head_count, head_width), (1, 0, 2)),
        (copies, 1, 1),
    )
    query_lanes = (lat_rows * head_width) // per_peer
    embed = query_lanes < lanes
    if not embed:
        query_lanes = 0
    row_dest = lax.broadcasted_iota(jnp.int32, (tok_rows,), 0) % cycle_size
    local_ids = (patch_of_row - row_dest * patches_dev).astype(jnp.bfloat16)
    id_lanes = jnp.pad(local_ids[:, None], ((0, 0), (0, lanes - query_lanes - 1)))
    payload = jnp.transpose(
        jnp.concatenate([tokens, id_lanes], axis=1).reshape(
            per_peer, cycle_size, model_width + lanes - query_lanes
        ),
        (1, 0, 2),
    )
    if embed:
        payload = jnp.concatenate(
            [payload, query_parts.reshape(cycle_size, per_peer, query_lanes)], axis=2
        )
        got = lax.all_to_all(payload, "blk", split_axis=0, concat_axis=0, tiled=True)
        got_queries = got[:, :, model_width + lanes - query_lanes :]
    else:
        got = lax.all_to_all(payload, "blk", split_axis=0, concat_axis=0, tiled=True)
        got_queries = lax.all_to_all(query_parts, "blk", split_axis=0, concat_axis=0, tiled=True)
    head_queries = lax.dynamic_slice_in_dim(
        got_queries, group_start, head_count, axis=0
    ).reshape(head_count * lat_rows, head_width)

    recv_rows = got[:, :, :model_width].reshape(CONTRASTS, patches_dev, model_width)
    recv_ids = got[:, :, model_width].astype(jnp.int32).reshape(CONTRASTS, 1, patches_dev)
    patch_iota = lax.broadcasted_iota(jnp.int32, (CONTRASTS, patches_dev, patches_dev), 1)
    selector = (recv_ids == patch_iota).astype(jnp.bfloat16)
    arranged = jnp.einsum(
        "cpk,ckd->cpd", selector, recv_rows, preferred_element_type=jnp.float32
    )
    joined = jnp.sum(arranged * contrast_gain.astype(jnp.float32)[:, None, :], axis=0)

    inverse_rms = lax.rsqrt(jnp.mean(joined * joined, axis=-1, keepdims=True) + 1e-05)
    normed = (joined * inverse_rms * norm_gain.astype(jnp.float32)).astype(jnp.bfloat16)
    pair_weight = jnp.concatenate(
        [
            w_key.reshape(model_width, head_count, head_width),
            w_value.reshape(model_width, head_count, head_width),
        ],
        axis=-1,
    )
    pair_rows = jnp.dot(
        normed,
        pair_weight.reshape(model_width, 2 * model_width),
        preferred_element_type=jnp.float32,
    ).astype(jnp.bfloat16)
    pair_rows = jnp.transpose(pair_rows.reshape(patches_dev, head_count, 2 * head_width), (1, 0, 2))
    got_pairs = lax.all_to_all(
        jnp.tile(pair_rows, (copies, 1, 1)), "blk", split_axis=0, concat_axis=0, tiled=True
    ).reshape(cycle_size * patches_dev, 2 * head_width)
    head_keys = got_pairs[:, :head_width]
    head_values = got_pairs[:, head_width:]

    scores = jnp.einsum(
        "ld,kd->lk", head_queries, head_keys, preferred_element_type=jnp.float32
    )
    maxima = jnp.max(scores, axis=-1, keepdims=True)
    weights = jnp.exp(scores - maxima)
    totals = jnp.sum(weights, axis=-1, keepdims=True)
    summed = jnp.dot(weights.astype(jnp.bfloat16), head_values, preferred_element_type=jnp.float32)
    attended_head = (summed / totals).astype(jnp.bfloat16).reshape(head_count, lat_rows, head_width)
    got_attended = lax.all_to_all(
        jnp.tile(attended_head, (copies, 1, 1)), "blk", split_axis=0, concat_axis=0, tiled=True
    )
    attended = jnp.transpose(
        lax.dynamic_slice_in_dim(got_attended, group_start, head_count, axis=0), (1, 0, 2)
    ).reshape(lat_rows, model_width)
    mixed = latents.astype(jnp.float32) + jnp.dot(
        attended, w_out, preferred_element_type=jnp.float32
    )
    return mixed.astype(jnp.bfloat16)


def solution(mesh):
    in_specs = (
        P(("grp", "blk"), None),
        P(("grp", "blk")),
        P("blk", None),
        P(),
        P(),
        P(),
        P(),
        P(),
        P(),
    )
    out_specs = P(("grp", "blk"), None)
    return jax.shard_map(local, mesh=mesh, in_specs=in_specs, out_specs=out_specs, check_vma=False)
```

```python
import jax
import jax.numpy as jnp
from jax import lax
from jax.sharding import Mesh
from jax.sharding import PartitionSpec as P

HEADS = 16
CONTRASTS = 4
SIDE = 8
BLK = ("side", "rest")


def split_exact(value, upward):
    high = value.astype(jnp.bfloat16)
    rest = value - high.astype(jnp.float32)
    if upward:
        rest = rest + jnp.abs(rest) * (2.0 ** -8)
    return high, rest.astype(jnp.bfloat16)


def local(tokens, patch_of_row, latents, contrast_gain, norm_gain, w_query, w_key, w_value, w_out):
    cycle_size = lax.axis_size(BLK)
    my_index = lax.axis_index(BLK)
    side_size = lax.axis_size("rest")
    sides = cycle_size // side_size
    tok_rows, model_width = tokens.shape
    head_count = HEADS
    head_width = model_width // head_count
    heads_dev = head_count // side_size
    pair_width = heads_dev * head_width
    lat_rows = latents.shape[0]
    all_lat = lat_rows * cycle_size
    per_peer = tok_rows // cycle_size
    patches_dev = tok_rows // CONTRASTS
    lanes = 128
    query_lanes = (lat_rows * pair_width) // per_peer

    queries = (
        jnp.dot(latents, w_query, preferred_element_type=jnp.float32) * head_width ** (-0.5)
    ).astype(jnp.bfloat16)
    query_parts = jnp.tile(
        jnp.transpose(queries.reshape(lat_rows, side_size, pair_width), (1, 0, 2)),
        (sides, 1, 1),
    )
    embed = query_lanes < lanes
    if not embed:
        query_lanes = 0
    row_dest = lax.broadcasted_iota(jnp.int32, (tok_rows,), 0) % cycle_size
    local_ids = (patch_of_row - row_dest * patches_dev).astype(jnp.bfloat16)
    id_lanes = jnp.pad(local_ids[:, None], ((0, 0), (0, lanes - query_lanes - 1)))
    payload = jnp.transpose(
        jnp.concatenate([tokens, id_lanes], axis=1).reshape(
            per_peer, cycle_size, model_width + lanes - query_lanes
        ),
        (1, 0, 2),
    )
    if embed:
        payload = jnp.concatenate(
            [payload, query_parts.reshape(cycle_size, per_peer, query_lanes)], axis=2
        )
        got = lax.all_to_all(payload, BLK, split_axis=0, concat_axis=0, tiled=True)
        got_queries = got[:, :, model_width + lanes - query_lanes :]
    else:
        got = lax.all_to_all(payload, BLK, split_axis=0, concat_axis=0, tiled=True)
        got_queries = lax.all_to_all(query_parts, BLK, split_axis=0, concat_axis=0, tiled=True)

    recv_rows = got[:, :, :model_width].reshape(CONTRASTS, patches_dev, model_width)
    recv_ids = got[:, :, model_width].astype(jnp.int32).reshape(CONTRASTS, 1, patches_dev)
    head_queries = jnp.transpose(
        got_queries.reshape(all_lat, heads_dev, head_width), (1, 0, 2)
    )
    patch_iota = lax.broadcasted_iota(jnp.int32, (CONTRASTS, patches_dev, patches_dev), 1)
    selector = (recv_ids == patch_iota).astype(jnp.bfloat16)
    arranged = jnp.einsum(
        "cpk,ckd->cpd", selector, recv_rows, preferred_element_type=jnp.float32
    )
    joined = jnp.sum(arranged * contrast_gain.astype(jnp.float32)[:, None, :], axis=0)

    inverse_rms = lax.rsqrt(jnp.mean(joined * joined, axis=-1, keepdims=True) + 1e-05)
    normed = (joined * inverse_rms * norm_gain.astype(jnp.float32)).astype(jnp.bfloat16)
    pair_weight = jnp.concatenate(
        [
            w_key.reshape(model_width, head_count, head_width),
            w_value.reshape(model_width, head_count, head_width),
        ],
        axis=-1,
    )
    pair_rows = jnp.dot(
        normed,
        pair_weight.reshape(model_width, 2 * model_width),
        preferred_element_type=jnp.float32,
    ).astype(jnp.bfloat16)
    pair_rows = jnp.transpose(
        pair_rows.reshape(patches_dev, side_size, heads_dev, 2 * head_width), (1, 2, 0, 3)
    ).reshape(side_size, heads_dev * patches_dev, 2 * head_width)
    got_pairs = lax.all_to_all(pair_rows, "rest", split_axis=0, concat_axis=0, tiled=True)
    got_pairs = jnp.transpose(
        got_pairs.reshape(side_size, heads_dev, patches_dev, 2 * head_width), (1, 0, 2, 3)
    ).reshape(heads_dev, side_size * patches_dev, 2 * head_width)
    head_keys = got_pairs[:, :, :head_width]
    head_values = got_pairs[:, :, head_width:]

    scores = jnp.einsum(
        "hld,hkd->hlk", head_queries, head_keys, preferred_element_type=jnp.float32
    )
    maxima = jnp.max(scores, axis=-1)
    max_high, max_low = split_exact(maxima, True)
    shift = max_high.astype(jnp.float32) + max_low.astype(jnp.float32)
    weights = jnp.exp(scores - shift[..., None])
    totals = jnp.sum(weights, axis=-1)
    tot_high, tot_low = split_exact(totals, False)
    summed = jnp.einsum(
        "hlk,hkd->lhd", weights.astype(jnp.bfloat16), head_values, preferred_element_type=jnp.float32
    ).astype(jnp.bfloat16)
    stats = jnp.transpose(jnp.stack([max_high, max_low, tot_high, tot_low], axis=-1), (1, 0, 2))
    part_payload = jnp.concatenate(
        [summed.reshape(all_lat, pair_width), stats.reshape(all_lat, heads_dev * 4)], axis=1
    ).reshape(cycle_size, lat_rows, pair_width + heads_dev * 4)
    got_parts = lax.all_to_all(part_payload, BLK, split_axis=0, concat_axis=0, tiled=True)
    got_parts = got_parts.astype(jnp.float32).reshape(sides, side_size, lat_rows, -1)
    part_sums = got_parts[..., :pair_width].reshape(
        sides, side_size, lat_rows, heads_dev, head_width
    )
    part_stats = got_parts[..., pair_width:].reshape(sides, side_size, lat_rows, heads_dev, 4)
    part_max = part_stats[..., 0] + part_stats[..., 1]
    part_tot = part_stats[..., 2] + part_stats[..., 3]
    top = jnp.max(part_max, axis=0)
    factor = jnp.exp(part_max - top[None])
    total = jnp.sum(part_tot * factor, axis=0)
    accum = jnp.sum(part_sums * factor[..., None], axis=0)
    attended = (accum / total[..., None]).astype(jnp.bfloat16)
    attended = jnp.transpose(attended, (1, 0, 2, 3)).reshape(lat_rows, model_width)
    mixed = latents.astype(jnp.float32) + jnp.dot(
        attended, w_out, preferred_element_type=jnp.float32
    )
    return mixed.astype(jnp.bfloat16)


def solution(mesh):
    groups, blocks = mesh.devices.shape
    side_mesh = Mesh(
        mesh.devices.reshape(groups, blocks // SIDE, SIDE), ("grp",) + BLK
    )
    rows = ("grp",) + BLK
    in_specs = (
        P(rows, None),
        P(rows),
        P(BLK, None),
        P(),
        P(),
        P(),
        P(),
        P(),
        P(),
    )
    out_specs = P(rows, None)
    return jax.shard_map(
        local, mesh=side_mesh, in_specs=in_specs, out_specs=out_specs, check_vma=False
    )
```

```python
import jax
import jax.numpy as jnp
from jax import lax
from jax.sharding import PartitionSpec as P

HEADS = 16
CONTRASTS = 4


def local(tokens, patch_of_row, latents, contrast_gain, norm_gain, w_query, w_key, w_value, w_out):
    cycle_size = lax.axis_size("blk")
    my_index = lax.axis_index("blk")
    tok_rows, model_width = tokens.shape
    head_count = HEADS
    head_width = model_width // head_count
    lat_rows = latents.shape[0]
    copies = cycle_size // head_count
    group_start = (my_index // head_count) * head_count
    per_peer = tok_rows // cycle_size
    patches_dev = tok_rows // CONTRASTS
    lanes = 128

    queries = (
        jnp.dot(latents, w_query, preferred_element_type=jnp.float32) * head_width ** (-0.5)
    ).astype(jnp.bfloat16)
    query_parts = jnp.tile(
        jnp.transpose(queries.reshape(lat_rows, head_count, head_width), (1, 0, 2)),
        (copies, 1, 1),
    )
    query_lanes = head_width
    embed = per_peer >= lat_rows and query_lanes < lanes
    if not embed:
        query_lanes = 0
    row_dest = lax.broadcasted_iota(jnp.int32, (tok_rows,), 0) % cycle_size
    local_ids = (patch_of_row - row_dest * patches_dev).astype(jnp.bfloat16)
    id_lanes = jnp.pad(local_ids[:, None], ((0, 0), (0, lanes - query_lanes - 1)))
    payload = jnp.transpose(
        jnp.concatenate([tokens, id_lanes], axis=1).reshape(
            per_peer, cycle_size, model_width + lanes - query_lanes
        ),
        (1, 0, 2),
    )
    if embed:
        query_rows = jnp.pad(query_parts, ((0, 0), (0, per_peer - lat_rows), (0, 0)))
        payload = jnp.concatenate([payload, query_rows], axis=2)
        got = lax.all_to_all(payload, "blk", split_axis=0, concat_axis=0, tiled=True)
        got_queries = got[:, :lat_rows, model_width + lanes - query_lanes :]
    else:
        got = lax.all_to_all(payload, "blk", split_axis=0, concat_axis=0, tiled=True)
        got_queries = lax.all_to_all(query_parts, "blk", split_axis=0, concat_axis=0, tiled=True)
    head_queries = lax.dynamic_slice_in_dim(
        got_queries, group_start, head_count, axis=0
    ).reshape(head_count * lat_rows, head_width)

    recv_rows = got[:, :, :model_width].reshape(CONTRASTS, patches_dev, model_width)
    recv_ids = got[:, :, model_width].astype(jnp.int32).reshape(CONTRASTS, 1, patches_dev)
    patch_iota = lax.broadcasted_iota(jnp.int32, (CONTRASTS, patches_dev, patches_dev), 1)
    selector = (recv_ids == patch_iota).astype(jnp.bfloat16)
    arranged = jnp.einsum(
        "cpk,ckd->cpd", selector, recv_rows, preferred_element_type=jnp.float32
    )
    joined = jnp.sum(arranged * contrast_gain.astype(jnp.float32)[:, None, :], axis=0)

    inverse_rms = lax.rsqrt(jnp.mean(joined * joined, axis=-1, keepdims=True) + 1e-05)
    normed = (joined * inverse_rms * norm_gain.astype(jnp.float32)).astype(jnp.bfloat16)
    pair_weight = jnp.concatenate(
        [
            w_key.reshape(model_width, head_count, head_width),
            w_value.reshape(model_width, head_count, head_width),
        ],
        axis=-1,
    )
    pair_rows = jnp.dot(
        normed,
        pair_weight.reshape(model_width, 2 * model_width),
        preferred_element_type=jnp.float32,
    ).astype(jnp.bfloat16)
    pair_rows = jnp.transpose(pair_rows.reshape(patches_dev, head_count, 2 * head_width), (1, 0, 2))
    got_pairs = lax.all_to_all(
        jnp.tile(pair_rows, (copies, 1, 1)), "blk", split_axis=0, concat_axis=0, tiled=True
    ).reshape(cycle_size * patches_dev, 2 * head_width)
    head_keys = got_pairs[:, :head_width]
    head_values = got_pairs[:, head_width:]

    scores = jnp.einsum(
        "ld,kd->lk", head_queries, head_keys, preferred_element_type=jnp.float32
    )
    maxima = jnp.max(scores, axis=-1, keepdims=True)
    weights = jnp.exp(scores - maxima)
    totals = jnp.sum(weights, axis=-1, keepdims=True)
    summed = jnp.dot(weights.astype(jnp.bfloat16), head_values, preferred_element_type=jnp.float32)
    attended_head = (summed / totals).astype(jnp.bfloat16).reshape(head_count, lat_rows, head_width)
    got_attended = lax.all_to_all(
        jnp.tile(attended_head, (copies, 1, 1)), "blk", split_axis=0, concat_axis=0, tiled=True
    )
    attended = jnp.transpose(
        lax.dynamic_slice_in_dim(got_attended, group_start, head_count, axis=0), (1, 0, 2)
    ).reshape(lat_rows, model_width)
    mixed = latents.astype(jnp.float32) + jnp.dot(
        attended, w_out, preferred_element_type=jnp.float32
    )
    return mixed.astype(jnp.bfloat16)


def solution(mesh):
    in_specs = (
        P(("grp", "blk"), None),
        P(("grp", "blk")),
        P("blk", None),
        P(),
        P(),
        P(),
        P(),
        P(),
        P(),
    )
    out_specs = P(("grp", "blk"), None)
    return jax.shard_map(local, mesh=mesh, in_specs=in_specs, out_specs=out_specs, check_vma=False)
```

```python
import jax
import jax.numpy as jnp
from jax import lax
from jax.experimental import pallas as pl
from jax.experimental.pallas import tpu as pltpu
from jax.sharding import PartitionSpec as P

HEADS = 16
CONTRASTS = 4


def pair_kernel(normed_ref, weight_ref, query_ref, out_ref):
    rows = normed_ref.shape[0]
    width = out_ref.shape[2]
    pairs = jnp.dot(
        normed_ref[...], weight_ref[...], preferred_element_type=jnp.float32
    ).astype(out_ref.dtype)
    for head in range(out_ref.shape[0]):
        out_ref[head, :rows, :] = pairs[:, head * width : (head + 1) * width]
        out_ref[head, rows:, :] = query_ref[head]


def pair_payload_of(normed, weight, query_parts):
    rows = normed.shape[0]
    heads, query_len, width = query_parts.shape
    in_vmem = pl.BlockSpec(memory_space=pltpu.VMEM)
    return pl.pallas_call(
        pair_kernel,
        out_shape=jax.ShapeDtypeStruct((heads, rows + query_len, width), normed.dtype),
        in_specs=[in_vmem, in_vmem, in_vmem],
        out_specs=in_vmem,
    )(normed, weight, query_parts)


def local(tokens, patch_of_row, latents, contrast_gain, norm_gain, w_query, w_key, w_value, w_out):
    cycle_size = lax.axis_size("blk")
    my_index = lax.axis_index("blk")
    tok_rows, model_width = tokens.shape
    head_count = HEADS
    head_width = model_width // head_count
    lat_rows = latents.shape[0]
    copies = cycle_size // head_count
    group_start = (my_index // head_count) * head_count
    per_peer = tok_rows // cycle_size
    patches_dev = tok_rows // CONTRASTS
    lanes = 128

    queries = (
        jnp.dot(latents, w_query, preferred_element_type=jnp.float32) * head_width ** (-0.5)
    ).astype(jnp.bfloat16)
    row_dest = lax.broadcasted_iota(jnp.int32, (tok_rows,), 0) % cycle_size
    local_ids = (patch_of_row - row_dest * patches_dev).astype(jnp.bfloat16)
    id_lanes = jnp.pad(local_ids[:, None], ((0, 0), (0, lanes - 1)))
    payload = jnp.transpose(
        jnp.concatenate([tokens, id_lanes], axis=1).reshape(
            per_peer, cycle_size, model_width + lanes
        ),
        (1, 0, 2),
    )
    got = lax.all_to_all(payload, "blk", split_axis=0, concat_axis=0, tiled=True)

    recv_rows = got[:, :, :model_width].reshape(CONTRASTS, patches_dev, model_width)
    recv_ids = got[:, :, model_width].astype(jnp.int32).reshape(CONTRASTS, 1, patches_dev)
    patch_iota = lax.broadcasted_iota(jnp.int32, (CONTRASTS, patches_dev, patches_dev), 1)
    selector = (recv_ids == patch_iota).astype(jnp.bfloat16)
    arranged = jnp.einsum(
        "cpk,ckd->cpd", selector, recv_rows, preferred_element_type=jnp.float32
    )
    joined = jnp.sum(arranged * contrast_gain.astype(jnp.float32)[:, None, :], axis=0)

    inverse_rms = lax.rsqrt(jnp.mean(joined * joined, axis=-1, keepdims=True) + 1e-05)
    normed = (joined * inverse_rms * norm_gain.astype(jnp.float32)).astype(jnp.bfloat16)
    pair_weight = jnp.concatenate(
        [
            w_key.reshape(model_width, head_count, head_width),
            w_value.reshape(model_width, head_count, head_width),
        ],
        axis=-1,
    )
    query_parts = jnp.transpose(queries.reshape(lat_rows, head_count, head_width), (1, 0, 2))
    query_parts = query_parts.reshape(head_count, -1, 2 * head_width)
    pair_payload = jnp.tile(
        pair_payload_of(normed, pair_weight.reshape(model_width, 2 * model_width), query_parts),
        (copies, 1, 1),
    )
    got_pairs = lax.all_to_all(pair_payload, "blk", split_axis=0, concat_axis=0, tiled=True)
    head_queries = lax.dynamic_slice_in_dim(
        got_pairs[:, patches_dev:], group_start, head_count, axis=0
    ).reshape(head_count * lat_rows, head_width)
    got_pairs = got_pairs[:, :patches_dev].reshape(cycle_size * patches_dev, 2 * head_width)
    head_keys = got_pairs[:, :head_width]
    head_values = got_pairs[:, head_width:]

    scores = jnp.einsum(
        "ld,kd->lk", head_queries, head_keys, preferred_element_type=jnp.float32
    )
    maxima = jnp.max(scores, axis=-1, keepdims=True)
    weights = jnp.exp(scores - maxima)
    totals = jnp.sum(weights, axis=-1, keepdims=True)
    summed = jnp.dot(weights.astype(jnp.bfloat16), head_values, preferred_element_type=jnp.float32)
    attended_head = (summed / totals).astype(jnp.bfloat16).reshape(head_count, lat_rows, head_width)
    got_attended = lax.all_to_all(
        jnp.tile(attended_head, (copies, 1, 1)), "blk", split_axis=0, concat_axis=0, tiled=True
    )
    attended = jnp.transpose(
        lax.dynamic_slice_in_dim(got_attended, group_start, head_count, axis=0), (1, 0, 2)
    ).reshape(lat_rows, model_width)
    mixed = latents.astype(jnp.float32) + jnp.dot(
        attended, w_out, preferred_element_type=jnp.float32
    )
    return mixed.astype(jnp.bfloat16)


def solution(mesh):
    in_specs = (
        P(("grp", "blk"), None),
        P(("grp", "blk")),
        P("blk", None),
        P(),
        P(),
        P(),
        P(),
        P(),
        P(),
    )
    out_specs = P(("grp", "blk"), None)
    return jax.shard_map(local, mesh=mesh, in_specs=in_specs, out_specs=out_specs, check_vma=False)
```

```python
import jax
import jax.numpy as jnp
from jax import lax
from jax.experimental import pallas as pl
from jax.experimental.pallas import tpu as pltpu
from jax.sharding import PartitionSpec as P

HEADS = 16
CONTRASTS = 4


def pair_kernel(joined_ref, gain_ref, weight_ref, query_ref, out_ref, normed_ref):
    rows = joined_ref.shape[0]
    width = out_ref.shape[2]

    @pl.when(pl.program_id(0) == 0)
    def _():
        joined = joined_ref[...]
        inverse_rms = lax.rsqrt(jnp.mean(joined * joined, axis=-1, keepdims=True) + 1e-05)
        normed_ref[...] = (joined * inverse_rms * gain_ref[...]).astype(normed_ref.dtype)

    pairs = jnp.dot(
        normed_ref[...], weight_ref[...], preferred_element_type=jnp.float32
    ).astype(out_ref.dtype)
    for head in range(out_ref.shape[0]):
        out_ref[head, :rows, :] = pairs[:, head * width : (head + 1) * width]
        out_ref[head, rows:, :] = query_ref[head]


def pair_payload_of(joined, gain, weight, query_parts):
    rows, model_width = joined.shape
    heads, query_len, width = query_parts.shape
    per_step = 2
    return pl.pallas_call(
        pair_kernel,
        out_shape=jax.ShapeDtypeStruct((heads, rows + query_len, width), weight.dtype),
        grid=(heads // per_step,),
        in_specs=[
            pl.BlockSpec((rows, model_width), lambda j: (0, 0)),
            pl.BlockSpec((1, model_width), lambda j: (0, 0)),
            pl.BlockSpec((model_width, per_step * width), lambda j: (0, j)),
            pl.BlockSpec((per_step, query_len, width), lambda j: (j, 0, 0)),
        ],
        out_specs=pl.BlockSpec((per_step, rows + query_len, width), lambda j: (j, 0, 0)),
        scratch_shapes=[pltpu.VMEM((rows, model_width), weight.dtype)],
        compiler_params=pltpu.CompilerParams(dimension_semantics=("arbitrary",)),
    )(joined, gain, weight, query_parts)


def local(tokens, patch_of_row, latents, contrast_gain, norm_gain, w_query, w_key, w_value, w_out):
    cycle_size = lax.axis_size("blk")
    my_index = lax.axis_index("blk")
    tok_rows, model_width = tokens.shape
    head_count = HEADS
    head_width = model_width // head_count
    lat_rows = latents.shape[0]
    copies = cycle_size // head_count
    group_start = (my_index // head_count) * head_count
    per_peer = tok_rows // cycle_size
    patches_dev = tok_rows // CONTRASTS
    lanes = 128

    queries = (
        jnp.dot(latents, w_query, preferred_element_type=jnp.float32) * head_width ** (-0.5)
    ).astype(jnp.bfloat16)
    row_dest = lax.broadcasted_iota(jnp.int32, (tok_rows,), 0) % cycle_size
    local_ids = (patch_of_row - row_dest * patches_dev).astype(jnp.bfloat16)
    id_lanes = jnp.pad(local_ids[:, None], ((0, 0), (0, lanes - 1)))
    payload = jnp.transpose(
        jnp.concatenate([tokens, id_lanes], axis=1).reshape(
            per_peer, cycle_size, model_width + lanes
        ),
        (1, 0, 2),
    )
    got = lax.all_to_all(payload, "blk", split_axis=0, concat_axis=0, tiled=True)

    recv_rows = got[:, :, :model_width].reshape(CONTRASTS, patches_dev, model_width)
    recv_ids = got[:, :, model_width].astype(jnp.int32).reshape(CONTRASTS, 1, patches_dev)
    patch_iota = lax.broadcasted_iota(jnp.int32, (CONTRASTS, patches_dev, patches_dev), 1)
    selector = (recv_ids == patch_iota).astype(jnp.bfloat16)
    arranged = jnp.einsum(
        "cpk,ckd->cpd", selector, recv_rows, preferred_element_type=jnp.float32
    )
    joined = jnp.sum(arranged * contrast_gain.astype(jnp.float32)[:, None, :], axis=0)

    pair_weight = jnp.concatenate(
        [
            w_key.reshape(model_width, head_count, head_width),
            w_value.reshape(model_width, head_count, head_width),
        ],
        axis=-1,
    )
    query_parts = jnp.transpose(queries.reshape(lat_rows, head_count, head_width), (1, 0, 2))
    query_parts = query_parts.reshape(head_count, -1, 2 * head_width)
    pair_payload = jnp.tile(
        pair_payload_of(
            joined,
            norm_gain.astype(jnp.float32).reshape(1, model_width),
            pair_weight.reshape(model_width, 2 * model_width),
            query_parts,
        ),
        (copies, 1, 1),
    )
    got_pairs = lax.all_to_all(pair_payload, "blk", split_axis=0, concat_axis=0, tiled=True)
    head_queries = lax.dynamic_slice_in_dim(
        got_pairs[:, patches_dev:], group_start, head_count, axis=0
    ).reshape(head_count * lat_rows, head_width)
    got_pairs = got_pairs[:, :patches_dev].reshape(cycle_size * patches_dev, 2 * head_width)
    head_keys = got_pairs[:, :head_width]
    head_values = got_pairs[:, head_width:]

    scores = jnp.einsum(
        "ld,kd->lk", head_queries, head_keys, preferred_element_type=jnp.float32
    )
    maxima = jnp.max(scores, axis=-1, keepdims=True)
    weights = jnp.exp(scores - maxima)
    totals = jnp.sum(weights, axis=-1, keepdims=True)
    summed = jnp.dot(weights.astype(jnp.bfloat16), head_values, preferred_element_type=jnp.float32)
    attended_head = (summed / totals).astype(jnp.bfloat16).reshape(head_count, lat_rows, head_width)
    got_attended = lax.all_to_all(
        jnp.tile(attended_head, (copies, 1, 1)), "blk", split_axis=0, concat_axis=0, tiled=True
    )
    attended = jnp.transpose(
        lax.dynamic_slice_in_dim(got_attended, group_start, head_count, axis=0), (1, 0, 2)
    ).reshape(lat_rows, model_width)
    mixed = latents.astype(jnp.float32) + jnp.dot(
        attended, w_out, preferred_element_type=jnp.float32
    )
    return mixed.astype(jnp.bfloat16)


def solution(mesh):
    in_specs = (
        P(("grp", "blk"), None),
        P(("grp", "blk")),
        P("blk", None),
        P(),
        P(),
        P(),
        P(),
        P(),
        P(),
    )
    out_specs = P(("grp", "blk"), None)
    return jax.shard_map(local, mesh=mesh, in_specs=in_specs, out_specs=out_specs, check_vma=False)
```
